128 devices in a mesh: dp: 16 (over x, y_lo, core), tensor: 8 (over z, y_hi).
Axes of the slice: x: 4, y: 4 (y_hi: 2, y_lo: 2; y = y_hi * 2 + y_lo), z: 4, core: 2. Of those that a mesh axis runs over, the one named last changes fastest.
Arguments:
- rows_in: bfloat16 [2048, 6144], P('dp'), may hold values from -6 to 6
- out_grad: bfloat16 [2048, 6144], P('dp'), may hold values from -1.5 to 1.5
- gate_pre: bfloat16 [2048, 12288], P('dp', 'tensor'), may hold values from -5 to 5
- up_pre: bfloat16 [2048, 12288], P('dp', 'tensor'), may hold values from -5 to 5
- w_gate: bfloat16 [2, 6144, 12288], P(None, 'dp', 'tensor'), may hold values from -0.078125 to 0.078125
- w_up: bfloat16 [2, 6144, 12288], P(None, 'dp', 'tensor'), may hold values from -0.078125 to 0.078125
- w_down: bfloat16 [2, 12288, 6144], P(None, 'tensor', 'dp'), may hold values from -0.0546875 to 0.0546875
- live_rows: int32 [16], P('dp'), may hold values from 32 to 128, as said below
- block_expert: int32 [16], replicated, may hold values from 0 to 1, as said below
Outputs:
- input_grad: bfloat16 [2048, 6144], P('dp', 'tensor')
- grad_gate: bfloat16 [2, 6144, 12288], P(None, 'dp', 'tensor')
- grad_up: bfloat16 [2, 6144, 12288], P(None, 'dp', 'tensor')
- grad_down: bfloat16 [2, 12288, 6144], P(None, 'tensor', 'dp')
The draws below stay inside these ranges and needn't reach their ends.
Inputs may be any that keep to these rules, and one draw needn't show every extreme that they name: `live_rows`: entry k counts the live rows among rank k's 128 rows; they come first and the rest are padding; some rank is full. `block_expert`: the expert of each aligned block of 128 rows; every expert owns at least one block.
All inputs are finite; a program needn't handle non-finite values.
Results may differ from the reference program's by a relative error of at most 0.005.
Values may be sent and summed in bfloat16 or wider, within the bound.
No kernel may reach another device: no remote copies, remote signals or barrier semaphores. Data moves between devices by JAX's collectives and lax.ppermute only.
A program may use at most 128 MiB of HBM per device.

```python
import jax
import jax.numpy as jnp
from jax import lax

D = 6144
FF = 12288
E_WIN = 2
BLOCK = 128
ROWS_DEV = 128
ROWS = 2048
NBLK = 16
N_DP = 16


def draw_live_rows(key, part):
    first, second = jax.random.split(key)
    third = jax.random.fold_in(key, 7)
    counts = jax.random.randint(first, (N_DP,), ROWS_DEV // 4, ROWS_DEV + 1)
    full_rank = jax.random.randint(second, (), 0, N_DP)
    low_rank = (full_rank + 1 + jax.random.randint(third, (), 0, N_DP - 1)) % N_DP
    ranks = jnp.arange(N_DP, dtype=jnp.int32)
    counts = jnp.where(ranks == low_rank, ROWS_DEV // 4, counts)
    counts = jnp.where(ranks == full_rank, ROWS_DEV, counts)
    return counts.astype(jnp.int32)


def draw_block_expert(key, part):
    first, second = jax.random.split(key)
    base_draw = jax.random.randint(first, (NBLK,), 0, E_WIN)
    shuffled = jax.random.permutation(second, NBLK)
    return jnp.where(shuffled < E_WIN, shuffled, base_draw).astype(jnp.int32)


def spiked(values, rng, source, target, parts, factor):
    owner, partner = [(jnp.arange(values.shape[axis_at]) // (values.shape[axis_at] // parts)).reshape([-1 if axis == axis_at else 1 for axis in range(values.ndim)]) for axis_at in (source, target)]
    chosen = jax.random.permutation(rng, parts)[partner]
    strong = (owner == chosen) | (owner == (partner + parts // 2) % parts)
    return jnp.where(strong, factor * values, values)


def steps_of(stream_key, extent, cuts, low, high):
    factor_of = 1.0
    for dim, parts in cuts:
        steps = jax.random.uniform(jax.random.fold_in(jax.random.fold_in(stream_key, 6), dim), (parts,), jnp.float32, low / len(cuts), high / len(cuts))
        factor_of = factor_of * jnp.repeat(jnp.exp(steps), extent[dim] // parts).reshape((-1,) + (1,) * (len(extent) - 1 - dim))
    return factor_of


def noise(own_key, shape, deviation, limit, cuts=(), kind=jnp.bfloat16):
    loudness = steps_of(own_key, shape, cuts, -0.22, 0.18) if cuts else 1.0
    array = jax.random.normal(own_key, shape, jnp.float32) * deviation * loudness
    return jnp.minimum(jnp.maximum(array, -limit), limit).astype(kind)


def noise_with(key, dims, spread, most, pieces, heavy, kind=jnp.bfloat16):
    values = spread * jax.random.normal(key, dims, jnp.float32)
    if pieces:
        values = values * steps_of(key, dims, pieces, -0.22, 0.18)
    return jnp.clip(spiked(values, jax.random.fold_in(key, 3), *heavy), -most, most).astype(kind)


def setup_inputs(seed: int = 0) -> dict:
    streams_of = jax.random.split(jax.random.key(seed), 10)
    rows_in = noise(streams_of[0], (ROWS, D), 1.0, 6.0, ((0, 16),))
    out_grad = noise_with(streams_of[1], (ROWS, D), 0.25, 1.5, ((0, 16),), (1, 0, 16, 2.0))
    gate_pre = noise(streams_of[2], (ROWS, FF), 1.0, 5.0, ((0, 16), (1, 8)))
    up_pre = noise(streams_of[3], (ROWS, FF), 1.0, 5.0, ((0, 16), (1, 8)))
    w_gate = noise(streams_of[4], (E_WIN, D, FF), D ** -0.5, 0.078125, ((1, 16), (2, 8)))
    w_up = noise(streams_of[5], (E_WIN, D, FF), D ** -0.5, 0.078125, ((1, 16), (2, 8)))
    w_down = noise(streams_of[6], (E_WIN, FF, D), FF ** -0.5, 0.0546875, ((1, 8), (2, 16)))
    live_rows = draw_live_rows(jax.random.fold_in(streams_of[9], 71), 0)
    block_expert = draw_block_expert(jax.random.fold_in(streams_of[9], 71), 0)
    return dict(rows_in=rows_in, out_grad=out_grad, gate_pre=gate_pre, up_pre=up_pre, w_gate=w_gate, w_up=w_up, w_down=w_down, live_rows=live_rows, block_expert=block_expert)


def contract_rows(left_op, right_op):
    return lax.dot_general(left_op, right_op, (((0,), (0,)), ((), ())), preferred_element_type=jnp.float32)


def contract_cols(left_op, right_op):
    return lax.dot_general(left_op, right_op, (((1,), (1,)), ((), ())), preferred_element_type=jnp.float32)


def reference(rows_in, out_grad, gate_pre, up_pre, w_gate, w_up, w_down, live_rows, block_expert):
    positions = jnp.arange(ROWS, dtype=jnp.int32)
    owners = positions // ROWS_DEV
    row_mask = ((positions % ROWS_DEV) < live_rows[owners]).astype(jnp.float32)[:, None]
    nblocks = ROWS // BLOCK

    def as_blocks(values_in):
        return values_in.reshape(nblocks, BLOCK, values_in.shape[-1])

    def one_block(totals, entries):
        x_rows, dy_rows, gate_rows, up_rows, mask_rows, expert = entries
        down_total, gate_total, up_total = totals
        weight_down = lax.dynamic_index_in_dim(w_down, expert, 0, keepdims=False)
        weight_gate = lax.dynamic_index_in_dim(w_gate, expert, 0, keepdims=False)
        weight_up = lax.dynamic_index_in_dim(w_up, expert, 0, keepdims=False)
        hidden_grad = contract_cols(dy_rows, weight_down)
        gate_vals = gate_rows.astype(jnp.float32)
        up_vals = up_rows.astype(jnp.float32)
        sigmoid = jax.nn.sigmoid(gate_vals)
        silu_vals = gate_vals * sigmoid
        hidden = (silu_vals * up_vals * mask_rows).astype(jnp.bfloat16)
        up_grad = (hidden_grad * silu_vals * mask_rows).astype(jnp.bfloat16)
        gate_grad = (hidden_grad * up_vals * sigmoid * (1.0 + gate_vals * (1.0 - sigmoid)) * mask_rows).astype(jnp.bfloat16)
        down_total = down_total.at[expert].add(contract_rows(hidden, dy_rows))
        gate_total = gate_total.at[expert].add(contract_rows(x_rows, gate_grad))
        up_total = up_total.at[expert].add(contract_rows(x_rows, up_grad))
        input_rows = contract_cols(gate_grad, weight_gate) + contract_cols(up_grad, weight_up)
        return (down_total, gate_total, up_total), input_rows.astype(jnp.bfloat16)

    initial = (jnp.zeros(w_down.shape, jnp.float32), jnp.zeros(w_gate.shape, jnp.float32), jnp.zeros(w_up.shape, jnp.float32))
    entries = (as_blocks(rows_in), as_blocks(out_grad), as_blocks(gate_pre), as_blocks(up_pre), row_mask.reshape(nblocks, BLOCK, 1), block_expert.astype(jnp.int32))
    totals, input_blocks = lax.scan(one_block, initial, entries)
    down_total, gate_total, up_total = totals
    return (input_blocks.reshape(ROWS, D), gate_total.astype(jnp.bfloat16), up_total.astype(jnp.bfloat16), down_total.astype(jnp.bfloat16))
```

```python
import numpy as np
import jax
import jax.numpy as jnp
from jax import lax
from jax.sharding import Mesh
from jax.sharding import PartitionSpec as P

BLOCK = 128
AXES = ("x", "ylo", "core", "z", "yhi")
SIZES = (4, 2, 2, 4, 2)
DP = ("x", "ylo", "core")
TP = ("z", "yhi")
CHIPS = ("x", "ylo")
N_DP = 16
N_TP = 8


def rank_of_pos(pos):
    core, x, ylo = pos // 8, (pos % 8) // 2, pos % 2
    return x * 4 + ylo * 2 + core


POS_RANK = np.array([rank_of_pos(p) for p in range(N_DP)], np.int32)


def deliver_perm(k):
    pairs = []
    for i in range(N_DP):
        for t in range(N_TP):
            dest = rank_of_pos(2 * t + ((i % 2) ^ k))
            pairs.append((i * N_TP + t, dest * N_TP + i // 2))
    return pairs


def contract_rows(left_op, right_op):
    return lax.dot_general(
        left_op, right_op, (((0,), (0,)), ((), ())), preferred_element_type=jnp.float32
    )


def contract_cols(left_op, right_op):
    return lax.dot_general(
        left_op, right_op, (((1,), (1,)), ((), ())), preferred_element_type=jnp.float32
    )


def expert_masks(block_expert, row_count, expert_count):
    spread = jnp.broadcast_to(block_expert[:, None], (row_count // BLOCK, BLOCK)).reshape(
        row_count, 1
    )
    return [(spread == which).astype(jnp.bfloat16) for which in range(expert_count)]


def to_gathered_order(cols):
    width = cols.shape[1]
    return cols.reshape(4, 2, 2, BLOCK, width).transpose(2, 0, 1, 3, 4).reshape(-1, width)


def shards(rows_in, out_grad, gate_pre, up_pre, w_gate, w_up, w_down, live_rows, block_expert):
    rows_dev = rows_in.shape[0]
    expert_count = w_gate.shape[0]
    ff = gate_pre.shape[1]
    dy_cols = to_gathered_order(
        lax.all_to_all(out_grad, DP, split_axis=1, concat_axis=0, tiled=True)
    )
    x_cols = to_gathered_order(
        lax.all_to_all(rows_in, DP, split_axis=1, concat_axis=0, tiled=True)
    )
    row_count = dy_cols.shape[0]
    expert_g = jnp.take(block_expert, jnp.asarray(POS_RANK), axis=0)
    masks = expert_masks(expert_g, row_count, expert_count)

    positions = jnp.arange(rows_dev, dtype=jnp.int32)[:, None]
    row_mask = (positions < live_rows[0]).astype(jnp.float32)
    gate_vals = gate_pre.astype(jnp.float32)
    up_vals = up_pre.astype(jnp.float32)
    sigmoid = jax.nn.sigmoid(gate_vals)
    silu_vals = gate_vals * sigmoid
    hidden = (silu_vals * up_vals * row_mask).astype(jnp.bfloat16)

    result = jnp.zeros((row_count, ff), jnp.float32)
    for which in range(expert_count):
        result = result + contract_cols(dy_cols * masks[which], w_down[which])
    result = lax.psum_scatter(
        result.reshape(2, row_count // 2, ff), "core", scatter_dimension=0, tiled=True
    ).reshape(row_count // 2, ff)
    hidden_grad = lax.psum_scatter(result, CHIPS, scatter_dimension=0, tiled=True)

    up_grad = (hidden_grad * silu_vals * row_mask).astype(jnp.bfloat16)
    gate_grad = (
        hidden_grad * up_vals * sigmoid * (1.0 + gate_vals * (1.0 - sigmoid)) * row_mask
    ).astype(jnp.bfloat16)
    packed = jnp.stack([hidden, gate_grad, up_grad], axis=1)
    packed = lax.all_gather(packed, CHIPS, axis=0, tiled=True)
    packed = lax.all_gather(packed, "core", axis=0, tiled=True)
    hid_g, gate_g, up_g = packed[:, 0], packed[:, 1], packed[:, 2]

    down_terms = []
    gate_terms = []
    up_terms = []
    partial_rows = jnp.zeros((row_count, w_gate.shape[1]), jnp.float32)
    for which in range(expert_count):
        down_terms.append(contract_rows(hid_g * masks[which], dy_cols))
        gate_masked = gate_g * masks[which]
        up_masked = up_g * masks[which]
        gate_terms.append(contract_rows(x_cols, gate_masked))
        up_terms.append(contract_rows(x_cols, up_masked))
        partial_rows = (
            partial_rows
            + contract_cols(gate_masked, w_gate[which])
            + contract_cols(up_masked, w_up[which])
        )
    down_total = jnp.stack(down_terms, 0)
    gate_total = jnp.stack(gate_terms, 0)
    up_total = jnp.stack(up_terms, 0)

    width = partial_rows.shape[1]
    summed = lax.psum_scatter(
        partial_rows.reshape(N_TP, row_count // N_TP, width), TP, scatter_dimension=0, tiled=True
    ).reshape(2, rows_dev, width)
    core = lax.axis_index("core")
    ylo = lax.axis_index("ylo")
    got = []
    for k in range(2):
        piece = lax.dynamic_index_in_dim(summed, core ^ k, 0, keepdims=False)
        got.append(lax.ppermute(piece, AXES, deliver_perm(k)))
    first = jnp.where(ylo == 0, got[0], got[1])
    second = jnp.where(ylo == 0, got[1], got[0])
    input_grad = jnp.concatenate([first, second], axis=1).astype(jnp.bfloat16)
    return (
        input_grad,
        gate_total.astype(jnp.bfloat16),
        up_total.astype(jnp.bfloat16),
        down_total.astype(jnp.bfloat16),
    )


def solution(mesh):
    fine = Mesh(mesh.devices.reshape(SIZES), AXES)
    return jax.shard_map(
        shards,
        mesh=fine,
        in_specs=(
            P(DP, None),
            P(DP, None),
            P(DP, TP),
            P(DP, TP),
            P(None, DP, TP),
            P(None, DP, TP),
            P(None, TP, DP),
            P(DP),
            P(),
        ),
        out_specs=(
            P(DP, TP),
            P(None, DP, TP),
            P(None, DP, TP),
            P(None, TP, DP),
        ),
        check_vma=False,
    )
```

```python
import numpy as np
import jax
import jax.numpy as jnp
from jax import lax
from jax.sharding import Mesh
from jax.sharding import PartitionSpec as P

BLOCK = 128
AXES = ("x", "ylo", "core", "z", "yhi")
SIZES = (4, 2, 2, 4, 2)
DP = ("x", "ylo", "core")
TP = ("z", "yhi")
CHIPS = ("x", "ylo")
N_DP = 16
N_TP = 8


def rank_of_pos(pos):
    core, x, ylo = pos // 8, (pos % 8) // 2, pos % 2
    return x * 4 + ylo * 2 + core


POS_RANK = np.array([rank_of_pos(p) for p in range(N_DP)], np.int32)


def deliver_perm(k):
    pairs = []
    for i in range(N_DP):
        for t in range(N_TP):
            dest = 2 * t + ((i % 2) ^ k)
            pairs.append((i * N_TP + t, dest * N_TP + i // 2))
    return pairs


def contract_rows(left_op, right_op):
    return lax.dot_general(
        left_op, right_op, (((0,), (0,)), ((), ())), preferred_element_type=jnp.float32
    )


def contract_cols(left_op, right_op):
    return lax.dot_general(
        left_op, right_op, (((1,), (1,)), ((), ())), preferred_element_type=jnp.float32
    )


def expert_masks(block_expert, row_count, expert_count):
    spread = jnp.broadcast_to(block_expert[:, None], (row_count // BLOCK, BLOCK)).reshape(
        row_count, 1
    )
    return [(spread == which).astype(jnp.bfloat16) for which in range(expert_count)]


def to_gathered_order(cols):
    width = cols.shape[1]
    return cols.reshape(4, 2, 2, BLOCK, width).transpose(2, 0, 1, 3, 4).reshape(-1, width)


def shards(rows_in, out_grad, gate_pre, up_pre, w_gate, w_up, w_down, live_rows, block_expert):
    rows_dev = rows_in.shape[0]
    expert_count = w_gate.shape[0]
    ff = gate_pre.shape[1]
    dy_cols = lax.all_to_all(out_grad, DP, split_axis=1, concat_axis=0, tiled=True)
    x_cols = lax.all_to_all(rows_in, DP, split_axis=1, concat_axis=0, tiled=True)
    row_count = dy_cols.shape[0]
    expert_g = jnp.take(block_expert, jnp.asarray(POS_RANK), axis=0)
    masks_g = expert_masks(expert_g, row_count, expert_count)
    masks = expert_masks(block_expert, row_count, expert_count)

    positions = jnp.arange(rows_dev, dtype=jnp.int32)[:, None]
    row_mask = (positions < live_rows[0]).astype(jnp.float32)
    gate_vals = gate_pre.astype(jnp.float32)
    up_vals = up_pre.astype(jnp.float32)
    sigmoid = jax.nn.sigmoid(gate_vals)
    silu_vals = gate_vals * sigmoid
    hidden = (silu_vals * up_vals * row_mask).astype(jnp.bfloat16)

    dy_g = to_gathered_order(dy_cols)
    result = jnp.zeros((row_count, ff), jnp.float32)
    for which in range(expert_count):
        result = result + contract_cols(dy_g * masks_g[which], w_down[which])
    result = lax.psum_scatter(
        result.reshape(2, row_count // 2, ff), "core", scatter_dimension=0, tiled=True
    ).reshape(N_DP // 2, rows_dev, ff)
    pieces = lax.all_to_all(
        result.astype(jnp.bfloat16), CHIPS, split_axis=0, concat_axis=0, tiled=True
    )
    hidden_grad = jnp.sum(pieces.astype(jnp.float32), axis=0)

    up_grad = (hidden_grad * silu_vals * row_mask).astype(jnp.bfloat16)
    gate_grad = (
        hidden_grad * up_vals * sigmoid * (1.0 + gate_vals * (1.0 - sigmoid)) * row_mask
    ).astype(jnp.bfloat16)
    packed = jnp.stack([hidden, gate_grad, up_grad], axis=1)
    packed = lax.all_gather(packed, DP, axis=0, tiled=True)
    hid_g, gate_g, up_g = packed[:, 0], packed[:, 1], packed[:, 2]

    down_terms = []
    gate_terms = []
    up_terms = []
    partial_rows = jnp.zeros((row_count, w_gate.shape[1]), jnp.float32)
    for which in range(expert_count):
        down_terms.append(contract_rows(hid_g * masks[which], dy_cols))
        gate_masked = gate_g * masks[which]
        up_masked = up_g * masks[which]
        gate_terms.append(contract_rows(x_cols, gate_masked))
        up_terms.append(contract_rows(x_cols, up_masked))
        partial_rows = (
            partial_rows
            + contract_cols(gate_masked, w_gate[which])
            + contract_cols(up_masked, w_up[which])
        )
    down_total = jnp.stack(down_terms, 0)
    gate_total = jnp.stack(gate_terms, 0)
    up_total = jnp.stack(up_terms, 0)

    width = partial_rows.shape[1]
    summed = lax.psum_scatter(
        partial_rows.reshape(N_TP, row_count // N_TP, width), TP, scatter_dimension=0, tiled=True
    ).reshape(2, rows_dev, width)
    core = lax.axis_index("core")
    got = []
    for k in range(2):
        piece = lax.dynamic_index_in_dim(summed, core ^ k, 0, keepdims=False)
        got.append(lax.ppermute(piece, AXES, deliver_perm(k)))
    first = jnp.where(core == 0, got[0], got[1])
    second = jnp.where(core == 0, got[1], got[0])
    input_grad = jnp.concatenate([first, second], axis=1).astype(jnp.bfloat16)
    return (
        input_grad,
        gate_total.astype(jnp.bfloat16),
        up_total.astype(jnp.bfloat16),
        down_total.astype(jnp.bfloat16),
    )


def solution(mesh):
    fine = Mesh(mesh.devices.reshape(SIZES), AXES)
    return jax.shard_map(
        shards,
        mesh=fine,
        in_specs=(
            P(DP, None),
            P(DP, None),
            P(DP, TP),
            P(DP, TP),
            P(None, DP, TP),
            P(None, DP, TP),
            P(None, TP, DP),
            P(DP),
            P(),
        ),
        out_specs=(
            P(DP, TP),
            P(None, DP, TP),
            P(None, DP, TP),
            P(None, TP, DP),
        ),
        check_vma=False,
    )
```

```python
import numpy as np
import jax
import jax.numpy as jnp
from jax import lax
from jax.sharding import Mesh
from jax.sharding import PartitionSpec as P

BLOCK = 128
AXES = ("x", "ylo", "core", "z", "yhi")
SIZES = (4, 2, 2, 4, 2)
DP = ("x", "ylo", "core")
TP = ("z", "yhi")
CHIPS = ("x", "ylo")
N_DP = 16
N_TP = 8


def rank_of_pos(pos):
    core, x, ylo = pos // 8, (pos % 8) // 2, pos % 2
    return x * 4 + ylo * 2 + core


POS_RANK = np.array([rank_of_pos(p) for p in range(N_DP)], np.int32)


def deliver_perm(k):
    pairs = []
    for i in range(N_DP):
        for t in range(N_TP):
            dest = 8 * ((i % 2) ^ k) + t
            pairs.append((i * N_TP + t, dest * N_TP + i // 2))
    return pairs


def contract_rows(left_op, right_op):
    return lax.dot_general(
        left_op, right_op, (((0,), (0,)), ((), ())), preferred_element_type=jnp.float32
    )


def contract_cols(left_op, right_op):
    return lax.dot_general(
        left_op, right_op, (((1,), (1,)), ((), ())), preferred_element_type=jnp.float32
    )


def expert_masks(block_expert, row_count, expert_count):
    spread = jnp.broadcast_to(block_expert[:, None], (row_count // BLOCK, BLOCK)).reshape(
        row_count, 1
    )
    return [(spread == which).astype(jnp.bfloat16) for which in range(expert_count)]


def to_gathered_order(cols):
    width = cols.shape[1]
    return cols.reshape(4, 2, 2, BLOCK, width).transpose(2, 0, 1, 3, 4).reshape(-1, width)


def shards(rows_in, out_grad, gate_pre, up_pre, w_gate, w_up, w_down, live_rows, block_expert):
    rows_dev = rows_in.shape[0]
    expert_count = w_gate.shape[0]
    ff = gate_pre.shape[1]
    dy_cols = lax.all_to_all(out_grad, DP, split_axis=1, concat_axis=0, tiled=True)
    x_cols = lax.all_to_all(rows_in, DP, split_axis=1, concat_axis=0, tiled=True)
    row_count = dy_cols.shape[0]
    expert_g = jnp.take(block_expert, jnp.asarray(POS_RANK), axis=0)
    masks_g = expert_masks(expert_g, row_count, expert_count)
    masks = expert_masks(block_expert, row_count, expert_count)

    positions = jnp.arange(rows_dev, dtype=jnp.int32)[:, None]
    row_mask = (positions < live_rows[0]).astype(jnp.float32)
    gate_vals = gate_pre.astype(jnp.float32)
    up_vals = up_pre.astype(jnp.float32)
    sigmoid = jax.nn.sigmoid(gate_vals)
    silu_vals = gate_vals * sigmoid
    hidden = (silu_vals * up_vals * row_mask).astype(jnp.bfloat16)
    hid_g = lax.all_gather(hidden, DP, axis=0, tiled=True)

    dy_g = to_gathered_order(dy_cols)
    result = jnp.zeros((row_count, ff), jnp.float32)
    for which in range(expert_count):
        result = result + contract_cols(dy_g * masks_g[which], w_down[which])
    result = lax.psum_scatter(
        result.reshape(2, row_count // 2, ff), "core", scatter_dimension=0, tiled=True
    ).reshape(N_DP // 2, rows_dev, ff)
    pieces = lax.all_to_all(result, CHIPS, split_axis=0, concat_axis=0, tiled=True)
    hidden_grad = jnp.sum(pieces, axis=0)

    up_grad = (hidden_grad * silu_vals * row_mask).astype(jnp.bfloat16)
    gate_grad = (
        hidden_grad * up_vals * sigmoid * (1.0 + gate_vals * (1.0 - sigmoid)) * row_mask
    ).astype(jnp.bfloat16)
    packed = jnp.stack([gate_grad, up_grad], axis=1)
    packed = lax.all_gather(packed, DP, axis=0, tiled=True)
    gate_g, up_g = packed[:, 0], packed[:, 1]

    down_terms = []
    gate_terms = []
    up_terms = []
    for which in range(expert_count):
        down_terms.append(contract_rows(hid_g * masks[which], dy_cols))
        gate_masked = gate_g * masks[which]
        up_masked = up_g * masks[which]
        gate_terms.append(contract_rows(x_cols, gate_masked))
        up_terms.append(contract_rows(x_cols, up_masked))
    down_total = jnp.stack(down_terms, 0)
    gate_total = jnp.stack(gate_terms, 0)
    up_total = jnp.stack(up_terms, 0)

    width = w_gate.shape[1]
    half_rows = row_count // 2
    summed = []
    for half in range(2):
        rows = slice(half * half_rows, (half + 1) * half_rows)
        partial_rows = jnp.zeros((half_rows, width), jnp.float32)
        for which in range(expert_count):
            gate_masked = gate_g[rows] * masks[which][rows]
            up_masked = up_g[rows] * masks[which][rows]
            partial_rows = (
                partial_rows
                + contract_cols(gate_masked, w_gate[which])
                + contract_cols(up_masked, w_up[which])
            )
        summed.append(
            lax.psum_scatter(
                partial_rows.reshape(N_TP, rows_dev, width), TP, scatter_dimension=0, tiled=True
            ).reshape(rows_dev, width)
        )
    summed = jnp.stack(summed, 0)
    core = lax.axis_index("core")
    low = lax.axis_index("x") < 2
    got = []
    for k in range(2):
        piece = lax.dynamic_index_in_dim(summed, core ^ k, 0, keepdims=False)
        got.append(lax.ppermute(piece, AXES, deliver_perm(k)))
    first = jnp.where(low, got[0], got[1])
    second = jnp.where(low, got[1], got[0])
    input_grad = jnp.concatenate([first, second], axis=1).astype(jnp.bfloat16)
    return (
        input_grad,
        gate_total.astype(jnp.bfloat16),
        up_total.astype(jnp.bfloat16),
        down_total.astype(jnp.bfloat16),
    )


def solution(mesh):
    fine = Mesh(mesh.devices.reshape(SIZES), AXES)
    return jax.shard_map(
        shards,
        mesh=fine,
        in_specs=(
            P(DP, None),
            P(DP, None),
            P(DP, TP),
            P(DP, TP),
            P(None, DP, TP),
            P(None, DP, TP),
            P(None, TP, DP),
            P(DP),
            P(),
        ),
        out_specs=(
            P(DP, TP),
            P(None, DP, TP),
            P(None, DP, TP),
            P(None, TP, DP),
        ),
        check_vma=False,
    )
```

```python
import numpy as np
import jax
import jax.numpy as jnp
from jax import lax
from jax.sharding import Mesh
from jax.sharding import PartitionSpec as P

BLOCK = 128
AXES = ("x", "ylo", "core", "z", "yhi")
SIZES = (4, 2, 2, 4, 2)
DP = ("x", "ylo", "core")
TP = ("z", "yhi")
CHIPS = ("x", "ylo")
N_DP = 16
N_TP = 8


def rank_of_pos(pos):
    core, x, ylo = pos // 8, (pos % 8) // 2, pos % 2
    return x * 4 + ylo * 2 + core


POS_RANK = np.array([rank_of_pos(p) for p in range(N_DP)], np.int32)


def deliver_perm(k):
    pairs = []
    for i in range(N_DP):
        for t in range(N_TP):
            dest = 8 * ((i % 2) ^ k) + t
            pairs.append((i * N_TP + t, dest * N_TP + i // 2))
    return pairs


def contract_rows(left_op, right_op):
    return lax.dot_general(
        left_op, right_op, (((0,), (0,)), ((), ())), preferred_element_type=jnp.float32
    )


def contract_cols(left_op, right_op):
    return lax.dot_general(
        left_op, right_op, (((1,), (1,)), ((), ())), preferred_element_type=jnp.float32
    )


def expert_masks(block_expert, row_count, expert_count):
    spread = jnp.broadcast_to(block_expert[:, None], (row_count // BLOCK, BLOCK)).reshape(
        row_count, 1
    )
    return [(spread == which).astype(jnp.bfloat16) for which in range(expert_count)]


def to_gathered_order(cols):
    width = cols.shape[1]
    return cols.reshape(4, 2, 2, BLOCK, width).transpose(2, 0, 1, 3, 4).reshape(-1, width)


def shards(rows_in, out_grad, gate_pre, up_pre, w_gate, w_up, w_down, live_rows, block_expert):
    rows_dev = rows_in.shape[0]
    expert_count = w_gate.shape[0]
    ff = gate_pre.shape[1]
    dy_cols = lax.all_to_all(out_grad, DP, split_axis=1, concat_axis=0, tiled=True)
    x_cols = lax.all_to_all(rows_in, DP, split_axis=1, concat_axis=0, tiled=True)
    row_count = dy_cols.shape[0]
    expert_g = jnp.take(block_expert, jnp.asarray(POS_RANK), axis=0)
    masks_g = expert_masks(expert_g, row_count, expert_count)
    masks = expert_masks(block_expert, row_count, expert_count)

    positions = jnp.arange(rows_dev, dtype=jnp.int32)[:, None]
    row_mask = (positions < live_rows[0]).astype(jnp.float32)
    gate_vals = gate_pre.astype(jnp.float32)
    up_vals = up_pre.astype(jnp.float32)
    sigmoid = jax.nn.sigmoid(gate_vals)
    silu_vals = gate_vals * sigmoid
    hidden = (silu_vals * up_vals * row_mask).astype(jnp.bfloat16)
    hid_g = lax.all_gather(hidden, DP, axis=0, tiled=True)
    hid_g, dy_cols = lax.optimization_barrier((hid_g, dy_cols))

    half_ff = ff // 2
    dy_g = to_gathered_order(dy_cols)
    part_a = jnp.zeros((row_count, half_ff), jnp.float32)
    part_b = jnp.zeros((row_count, half_ff), jnp.float32)
    for which in range(expert_count):
        part_a = part_a + contract_cols(dy_cols * masks[which], w_down[which, :half_ff])
        part_b = part_b + contract_cols(dy_g * masks_g[which], w_down[which, half_ff:])
    part_b = lax.psum_scatter(
        part_b.reshape(2, row_count // 2, half_ff), "core", scatter_dimension=0, tiled=True
    ).reshape(N_DP // 2, rows_dev, half_ff)
    part_a, part_b = lax.optimization_barrier((part_a, part_b))
    grad_a = lax.psum_scatter(part_a, DP, scatter_dimension=0, tiled=True)
    pieces = lax.all_to_all(part_b, CHIPS, split_axis=0, concat_axis=0, tiled=True)
    hidden_grad = jnp.concatenate([grad_a, jnp.sum(pieces, axis=0)], axis=1)

    up_grad = (hidden_grad * silu_vals * row_mask).astype(jnp.bfloat16)
    gate_grad = (
        hidden_grad * up_vals * sigmoid * (1.0 + gate_vals * (1.0 - sigmoid)) * row_mask
    ).astype(jnp.bfloat16)
    packed = jnp.stack([gate_grad, up_grad], axis=1)
    packed = lax.all_gather(packed, DP, axis=0, tiled=True)
    gate_g, up_g = packed[:, 0], packed[:, 1]

    down_terms = []
    gate_terms = []
    up_terms = []
    for which in range(expert_count):
        down_terms.append(contract_rows(hid_g * masks[which], dy_cols))
        gate_masked = gate_g * masks[which]
        up_masked = up_g * masks[which]
        gate_terms.append(contract_rows(x_cols, gate_masked))
        up_terms.append(contract_rows(x_cols, up_masked))
    down_total = jnp.stack(down_terms, 0)
    gate_total = jnp.stack(gate_terms, 0)
    up_total = jnp.stack(up_terms, 0)

    width = w_gate.shape[1]
    half_rows = row_count // 2
    summed = []
    for half in range(2):
        rows = slice(half * half_rows, (half + 1) * half_rows)
        partial_rows = jnp.zeros((half_rows, width), jnp.float32)
        for which in range(expert_count):
            gate_masked = gate_g[rows] * masks[which][rows]
            up_masked = up_g[rows] * masks[which][rows]
            partial_rows = (
                partial_rows
                + contract_cols(gate_masked, w_gate[which])
                + contract_cols(up_masked, w_up[which])
            )
        pieces = lax.all_to_all(
            partial_rows.reshape(N_TP, rows_dev, width), TP, split_axis=0, concat_axis=0, tiled=True
        )
        summed.append(jnp.sum(pieces, axis=0))
    summed = jnp.stack(summed, 0)
    core = lax.axis_index("core")
    low = lax.axis_index("x") < 2
    got = []
    for k in range(2):
        piece = lax.dynamic_index_in_dim(summed, core ^ k, 0, keepdims=False)
        got.append(lax.ppermute(piece, AXES, deliver_perm(k)))
    first = jnp.where(low, got[0], got[1])
    second = jnp.where(low, got[1], got[0])
    input_grad = jnp.concatenate([first, second], axis=1).astype(jnp.bfloat16)
    return (
        input_grad,
        gate_total.astype(jnp.bfloat16),
        up_total.astype(jnp.bfloat16),
        down_total.astype(jnp.bfloat16),
    )


def solution(mesh):
    fine = Mesh(mesh.devices.reshape(SIZES), AXES)
    return jax.shard_map(
        shards,
        mesh=fine,
        in_specs=(
            P(DP, None),
            P(DP, None),
            P(DP, TP),
            P(DP, TP),
            P(None, DP, TP),
            P(None, DP, TP),
            P(None, TP, DP),
            P(DP),
            P(),
        ),
        out_specs=(
            P(DP, TP),
            P(None, DP, TP),
            P(None, DP, TP),
            P(None, TP, DP),
        ),
        check_vma=False,
    )
```

```python
import numpy as np
import jax
import jax.numpy as jnp
from jax import lax
from jax.sharding import Mesh
from jax.sharding import PartitionSpec as P

BLOCK = 128
AXES = ("x", "ylo", "core", "z", "yhi")
SIZES = (4, 2, 2, 4, 2)
DP = ("x", "ylo", "core")
TP = ("z", "yhi")
CHIPS = ("x", "ylo")
N_DP = 16
N_TP = 8


def rank_of_pos(pos):
    core, x, ylo = pos // 8, (pos % 8) // 2, pos % 2
    return x * 4 + ylo * 2 + core


POS_RANK = np.array([rank_of_pos(p) for p in range(N_DP)], np.int32)


def deliver_perm(k):
    pairs = []
    for i in range(N_DP):
        for t in range(N_TP):
            dest = 8 * ((i % 2) ^ k) + t
            pairs.append((i * N_TP + t, dest * N_TP + i // 2))
    return pairs


def contract_rows(left_op, right_op):
    return lax.dot_general(
        left_op, right_op, (((0,), (0,)), ((), ())), preferred_element_type=jnp.float32
    )


def contract_cols(left_op, right_op):
    return lax.dot_general(
        left_op, right_op, (((1,), (1,)), ((), ())), preferred_element_type=jnp.float32
    )


def expert_masks(block_expert, row_count, expert_count):
    spread = jnp.broadcast_to(block_expert[:, None], (row_count // BLOCK, BLOCK)).reshape(
        row_count, 1
    )
    return [(spread == which).astype(jnp.bfloat16) for which in range(expert_count)]


def to_gathered_order(cols):
    width = cols.shape[1]
    return cols.reshape(4, 2, 2, BLOCK, width).transpose(2, 0, 1, 3, 4).reshape(-1, width)


def shards(rows_in, out_grad, gate_pre, up_pre, w_gate, w_up, w_down, live_rows, block_expert):
    rows_dev = rows_in.shape[0]
    expert_count = w_gate.shape[0]
    ff = gate_pre.shape[1]
    dy_cols = lax.all_to_all(out_grad, DP, split_axis=1, concat_axis=0, tiled=True)
    x_cols = lax.all_to_all(rows_in, DP, split_axis=1, concat_axis=0, tiled=True)
    row_count = dy_cols.shape[0]
    expert_g = jnp.take(block_expert, jnp.asarray(POS_RANK), axis=0)
    masks_g = expert_masks(expert_g, row_count, expert_count)
    masks = expert_masks(block_expert, row_count, expert_count)

    positions = jnp.arange(rows_dev, dtype=jnp.int32)[:, None]
    row_mask = (positions < live_rows[0]).astype(jnp.float32)
    gate_vals = gate_pre.astype(jnp.float32)
    up_vals = up_pre.astype(jnp.float32)
    sigmoid = jax.nn.sigmoid(gate_vals)
    silu_vals = gate_vals * sigmoid
    hidden = (silu_vals * up_vals * row_mask).astype(jnp.bfloat16)
    hid_g = lax.all_gather(hidden, DP, axis=0, tiled=True)
    hid_g, dy_cols = lax.optimization_barrier((hid_g, dy_cols))

    dy_g = to_gathered_order(dy_cols)
    result = jnp.zeros((row_count, ff), jnp.float32)
    for which in range(expert_count):
        result = result + contract_cols(dy_g * masks_g[which], w_down[which])
    result = lax.psum_scatter(
        result.reshape(2, row_count // 2, ff), "core", scatter_dimension=0, tiled=True
    ).reshape(N_DP // 2, rows_dev, ff)
    xi = lax.axis_index("x")
    yi = lax.axis_index("ylo")
    hidden_grad = lax.dynamic_index_in_dim(result, xi * 2 + yi, 0, keepdims=False)
    for dx in range(4):
        for dy in range(2):
            if dx == 0 and dy == 0:
                continue
            dest = ((xi + dx) % 4) * 2 + (yi + dy) % 2
            piece = lax.dynamic_index_in_dim(result, dest, 0, keepdims=False)
            perm = [
                (x * 2 + y, ((x + dx) % 4) * 2 + (y + dy) % 2) for x in range(4) for y in range(2)
            ]
            hidden_grad = hidden_grad + lax.ppermute(piece, CHIPS, perm)

    up_grad = (hidden_grad * silu_vals * row_mask).astype(jnp.bfloat16)
    gate_grad = (
        hidden_grad * up_vals * sigmoid * (1.0 + gate_vals * (1.0 - sigmoid)) * row_mask
    ).astype(jnp.bfloat16)
    packed = jnp.stack([gate_grad, up_grad], axis=1)
    packed = lax.all_gather(packed, DP, axis=0, tiled=True)
    gate_g, up_g = packed[:, 0], packed[:, 1]

    down_terms = []
    gate_terms = []
    up_terms = []
    for which in range(expert_count):
        down_terms.append(contract_rows(hid_g * masks[which], dy_cols))
        gate_masked = gate_g * masks[which]
        up_masked = up_g * masks[which]
        gate_terms.append(contract_rows(x_cols, gate_masked))
        up_terms.append(contract_rows(x_cols, up_masked))
    down_total = jnp.stack(down_terms, 0)
    gate_total = jnp.stack(gate_terms, 0)
    up_total = jnp.stack(up_terms, 0)

    width = w_gate.shape[1]
    half_rows = row_count // 2
    summed = []
    for half in range(2):
        rows = slice(half * half_rows, (half + 1) * half_rows)
        partial_rows = jnp.zeros((half_rows, width), jnp.float32)
        for which in range(expert_count):
            gate_masked = gate_g[rows] * masks[which][rows]
            up_masked = up_g[rows] * masks[which][rows]
            partial_rows = (
                partial_rows
                + contract_cols(gate_masked, w_gate[which])
                + contract_cols(up_masked, w_up[which])
            )
        pieces = lax.all_to_all(
            partial_rows.reshape(N_TP, rows_dev, width), TP, split_axis=0, concat_axis=0, tiled=True
        )
        summed.append(jnp.sum(pieces, axis=0))
    summed = jnp.stack(summed, 0)
    core = lax.axis_index("core")
    low = lax.axis_index("x") < 2
    got = []
    for k in range(2):
        piece = lax.dynamic_index_in_dim(summed, core ^ k, 0, keepdims=False)
        got.append(lax.ppermute(piece, AXES, deliver_perm(k)))
    first = jnp.where(low, got[0], got[1])
    second = jnp.where(low, got[1], got[0])
    input_grad = jnp.concatenate([first, second], axis=1).astype(jnp.bfloat16)
    return (
        input_grad,
        gate_total.astype(jnp.bfloat16),
        up_total.astype(jnp.bfloat16),
        down_total.astype(jnp.bfloat16),
    )


def solution(mesh):
    fine = Mesh(mesh.devices.reshape(SIZES), AXES)
    return jax.shard_map(
        shards,
        mesh=fine,
        in_specs=(
            P(DP, None),
            P(DP, None),
            P(DP, TP),
            P(DP, TP),
            P(None, DP, TP),
            P(None, DP, TP),
            P(None, TP, DP),
            P(DP),
            P(),
        ),
        out_specs=(
            P(DP, TP),
            P(None, DP, TP),
            P(None, DP, TP),
            P(None, TP, DP),
        ),
        check_vma=False,
    )
```

```python
import numpy as np
import jax
import jax.numpy as jnp
from jax import lax
from jax.sharding import Mesh
from jax.sharding import PartitionSpec as P
from jax.experimental import pallas as pl
from jax.experimental.pallas import tpu as pltpu

BLOCK = 128
AXES = ("x", "ylo", "core", "z", "yhi")
SIZES = (4, 2, 2, 4, 2)
DP = ("x", "ylo", "core")
TP = ("z", "yhi")
CHIPS = ("x", "ylo")
N_DP = 16
N_TP = 8


def rank_of_pos(pos):
    core, x, ylo = pos // 8, (pos % 8) // 2, pos % 2
    return x * 4 + ylo * 2 + core


POS_RANK = np.array([rank_of_pos(p) for p in range(N_DP)], np.int32)


def deliver_perm(k):
    pairs = []
    for i in range(N_DP):
        for t in range(N_TP):
            dest = 8 * ((i % 2) ^ k) + t
            pairs.append((i * N_TP + t, dest * N_TP + i // 2))
    return pairs


def _cols_kernel(be_ref, *refs):
    n = (len(refs) - 1) // 2
    o_ref = refs[-1]
    acc = None
    for a in range(n):
        term = lax.dot_general(
            refs[2 * a][...], refs[2 * a + 1][...], (((1,), (1,)), ((), ())),
            preferred_element_type=jnp.float32,
        )
        acc = term if acc is None else acc + term
    o_ref[...] = acc


def grouped_cols(block_expert, pairs, width, part=0, first=0, blocks=None):
    rows0 = pairs[0][0]
    if blocks is None:
        blocks = rows0.shape[0] // BLOCK
    in_specs = []
    args = []
    for rows, w in pairs:
        in_specs.append(pl.BlockSpec((BLOCK, rows.shape[1]), lambda b, be: (b + first, 0)))
        in_specs.append(
            pl.BlockSpec((None, width, w.shape[2]), lambda b, be: (be[b + first], part, 0))
        )
        args += [rows, w]
    return pl.pallas_call(
        _cols_kernel,
        grid_spec=pltpu.PrefetchScalarGridSpec(
            num_scalar_prefetch=1,
            grid=(blocks,),
            in_specs=in_specs,
            out_specs=pl.BlockSpec((BLOCK, width), lambda b, be: (b, 0)),
        ),
        out_shape=jax.ShapeDtypeStruct((blocks * BLOCK, width), jnp.float32),
    )(block_expert, *args)


def _rows_kernel(order_ref, es_ref, *refs):
    n = len(refs) // 3
    b = pl.program_id(0)
    first = jnp.logical_or(b == 0, es_ref[b] != es_ref[jnp.maximum(b - 1, 0)])
    for a in range(n):
        left, right, o_ref = refs[a], refs[n + a], refs[2 * n + a]
        term = lax.dot_general(
            left[...], right[...], (((0,), (0,)), ((), ())), preferred_element_type=jnp.float32
        )

        @pl.when(first)
        def _():
            o_ref[...] = term

        @pl.when(jnp.logical_not(first))
        def _():
            o_ref[...] += term


def grouped_rows(block_expert, expert_count, lefts, rights):
    order = jnp.argsort(block_expert, stable=True).astype(jnp.int32)
    es = jnp.take(block_expert, order, axis=0)
    row_count = lefts[0].shape[0]
    in_specs = [pl.BlockSpec((BLOCK, l.shape[1]), lambda b, o, e: (o[b], 0)) for l in lefts]
    in_specs += [pl.BlockSpec((BLOCK, r.shape[1]), lambda b, o, e: (o[b], 0)) for r in rights]
    out_specs = [
        pl.BlockSpec((None, l.shape[1], r.shape[1]), lambda b, o, e: (e[b], 0, 0))
        for l, r in zip(lefts, rights)
    ]
    out_shape = [
        jax.ShapeDtypeStruct((expert_count, l.shape[1], r.shape[1]), jnp.float32)
        for l, r in zip(lefts, rights)
    ]
    return pl.pallas_call(
        _rows_kernel,
        grid_spec=pltpu.PrefetchScalarGridSpec(
            num_scalar_prefetch=2,
            grid=(row_count // BLOCK,),
            in_specs=in_specs,
            out_specs=out_specs,
        ),
        out_shape=out_shape,
    )(order, es, *lefts, *rights)


def contract_rows(left_op, right_op):
    return lax.dot_general(
        left_op, right_op, (((0,), (0,)), ((), ())), preferred_element_type=jnp.float32
    )


def contract_cols(left_op, right_op):
    return lax.dot_general(
        left_op, right_op, (((1,), (1,)), ((), ())), preferred_element_type=jnp.float32
    )


def expert_masks(block_expert, row_count, expert_count):
    spread = jnp.broadcast_to(block_expert[:, None], (row_count // BLOCK, BLOCK)).reshape(
        row_count, 1
    )
    return [(spread == which).astype(jnp.bfloat16) for which in range(expert_count)]


def to_gathered_order(cols):
    width = cols.shape[1]
    return cols.reshape(4, 2, 2, BLOCK, width).transpose(2, 0, 1, 3, 4).reshape(-1, width)


def shards(rows_in, out_grad, gate_pre, up_pre, w_gate, w_up, w_down, live_rows, block_expert):
    rows_dev = rows_in.shape[0]
    expert_count = w_gate.shape[0]
    ff = gate_pre.shape[1]
    dy_cols = lax.all_to_all(out_grad, DP, split_axis=1, concat_axis=0, tiled=True)
    x_cols = lax.all_to_all(rows_in, DP, split_axis=1, concat_axis=0, tiled=True)
    row_count = dy_cols.shape[0]
    expert_g = jnp.take(block_expert, jnp.asarray(POS_RANK), axis=0)

    positions = jnp.arange(rows_dev, dtype=jnp.int32)[:, None]
    row_mask = (positions < live_rows[0]).astype(jnp.float32)
    gate_vals = gate_pre.astype(jnp.float32)
    up_vals = up_pre.astype(jnp.float32)
    sigmoid = jax.nn.sigmoid(gate_vals)
    silu_vals = gate_vals * sigmoid
    hidden = (silu_vals * up_vals * row_mask).astype(jnp.bfloat16)
    hid_g = lax.all_gather(hidden, DP, axis=0, tiled=True)
    hid_g, dy_cols = lax.optimization_barrier((hid_g, dy_cols))

    half_ff = ff // 2
    dy_g = to_gathered_order(dy_cols)
    part_a = grouped_cols(block_expert, [(dy_cols, w_down)], half_ff, part=0)
    part_b = grouped_cols(expert_g, [(dy_g, w_down)], half_ff, part=1)
    part_b = lax.psum_scatter(
        part_b.reshape(2, row_count // 2, half_ff), "core", scatter_dimension=0, tiled=True
    ).reshape(N_DP // 2, rows_dev, half_ff)
    part_a, part_b = lax.optimization_barrier((part_a, part_b))
    grad_a = lax.psum_scatter(part_a, DP, scatter_dimension=0, tiled=True)
    pieces = lax.all_to_all(part_b, CHIPS, split_axis=0, concat_axis=0, tiled=True)
    hidden_grad = jnp.concatenate([grad_a, jnp.sum(pieces, axis=0)], axis=1)

    up_grad = (hidden_grad * silu_vals * row_mask).astype(jnp.bfloat16)
    gate_grad = (
        hidden_grad * up_vals * sigmoid * (1.0 + gate_vals * (1.0 - sigmoid)) * row_mask
    ).astype(jnp.bfloat16)
    packed = jnp.stack([gate_grad, up_grad], axis=1)
    packed = lax.all_gather(packed, DP, axis=0, tiled=True)
    gate_g, up_g = packed[:, 0], packed[:, 1]

    (down_total,) = grouped_rows(block_expert, expert_count, [hid_g], [dy_cols])
    gate_total, up_total = grouped_rows(
        block_expert, expert_count, [x_cols, x_cols], [gate_g, up_g]
    )

    width = w_gate.shape[1]
    half_blocks = row_count // BLOCK // 2
    summed = []
    for half in range(2):
        partial_rows = grouped_cols(
            block_expert,
            [(gate_g, w_gate), (up_g, w_up)],
            width,
            first=half * half_blocks,
            blocks=half_blocks,
        )
        pieces = lax.all_to_all(
            partial_rows.reshape(N_TP, rows_dev, width), TP, split_axis=0, concat_axis=0, tiled=True
        )
        summed.append(jnp.sum(pieces, axis=0))
    summed = jnp.stack(summed, 0)
    core = lax.axis_index("core")
    low = lax.axis_index("x") < 2
    got = []
    for k in range(2):
        piece = lax.dynamic_index_in_dim(summed, core ^ k, 0, keepdims=False)
        got.append(lax.ppermute(piece, AXES, deliver_perm(k)))
    first = jnp.where(low, got[0], got[1])
    second = jnp.where(low, got[1], got[0])
    input_grad = jnp.concatenate([first, second], axis=1).astype(jnp.bfloat16)
    return (
        input_grad,
        gate_total.astype(jnp.bfloat16),
        up_total.astype(jnp.bfloat16),
        down_total.astype(jnp.bfloat16),
    )


def solution(mesh):
    fine = Mesh(mesh.devices.reshape(SIZES), AXES)
    return jax.shard_map(
        shards,
        mesh=fine,
        in_specs=(
            P(DP, None),
            P(DP, None),
            P(DP, TP),
            P(DP, TP),
            P(None, DP, TP),
            P(None, DP, TP),
            P(None, TP, DP),
            P(DP),
            P(),
        ),
        out_specs=(
            P(DP, TP),
            P(None, DP, TP),
            P(None, DP, TP),
            P(None, TP, DP),
        ),
        check_vma=False,
    )
```

```python
import numpy as np
import jax
import jax.numpy as jnp
from jax import lax
from jax.sharding import Mesh
from jax.sharding import PartitionSpec as P

BLOCK = 128
AXES = ("x", "ylo", "core", "z", "yhi")
SIZES = (4, 2, 2, 4, 2)
DP = ("x", "ylo", "core")
TP = ("z", "yhi")
CHIPS = ("x", "ylo")
N_DP = 16
N_TP = 8


def rank_of_pos(pos):
    core, x, ylo = pos // 8, (pos % 8) // 2, pos % 2
    return x * 4 + ylo * 2 + core


POS_RANK = np.array([rank_of_pos(p) for p in range(N_DP)], np.int32)


def deliver_perm(k):
    pairs = []
    for i in range(N_DP):
        for t in range(N_TP):
            dest = 8 * ((i % 2) ^ k) + t
            pairs.append((i * N_TP + t, dest * N_TP + i // 2))
    return pairs


def contract_rows(left_op, right_op):
    return lax.dot_general(
        left_op, right_op, (((0,), (0,)), ((), ())), preferred_element_type=jnp.float32
    )


def contract_cols(left_op, right_op):
    return lax.dot_general(
        left_op, right_op, (((1,), (1,)), ((), ())), preferred_element_type=jnp.float32
    )


def expert_masks(block_expert, row_count, expert_count):
    spread = jnp.broadcast_to(block_expert[:, None], (row_count // BLOCK, BLOCK)).reshape(
        row_count, 1
    )
    return [(spread == which).astype(jnp.bfloat16) for which in range(expert_count)]


def to_gathered_order(cols):
    width = cols.shape[1]
    return cols.reshape(4, 2, 2, BLOCK, width).transpose(2, 0, 1, 3, 4).reshape(-1, width)


def shards(rows_in, out_grad, gate_pre, up_pre, w_gate, w_up, w_down, live_rows, block_expert):
    rows_dev = rows_in.shape[0]
    expert_count = w_gate.shape[0]
    ff = gate_pre.shape[1]
    dy_cols = lax.all_to_all(out_grad, DP, split_axis=1, concat_axis=0, tiled=True)
    x_cols = lax.all_to_all(rows_in, DP, split_axis=1, concat_axis=0, tiled=True)
    row_count = dy_cols.shape[0]
    expert_g = jnp.take(block_expert, jnp.asarray(POS_RANK), axis=0)
    masks_g = expert_masks(expert_g, row_count, expert_count)
    masks = expert_masks(block_expert, row_count, expert_count)

    positions = jnp.arange(rows_dev, dtype=jnp.int32)[:, None]
    row_mask = (positions < live_rows[0]).astype(jnp.float32)
    gate_vals = gate_pre.astype(jnp.float32)
    up_vals = up_pre.astype(jnp.float32)
    sigmoid = jax.nn.sigmoid(gate_vals)
    silu_vals = gate_vals * sigmoid
    hidden = (silu_vals * up_vals * row_mask).astype(jnp.bfloat16)
    hid_g = lax.all_gather(hidden, DP, axis=0, tiled=True)
    hid_g, dy_cols = lax.optimization_barrier((hid_g, dy_cols))

    half_ff = ff // 3
    dy_g = to_gathered_order(dy_cols)
    part_a = jnp.zeros((row_count, half_ff), jnp.float32)
    part_b = jnp.zeros((row_count, ff - half_ff), jnp.float32)
    for which in range(expert_count):
        part_a = part_a + contract_cols(dy_cols * masks[which], w_down[which, :half_ff])
        part_b = part_b + contract_cols(dy_g * masks_g[which], w_down[which, half_ff:])
    part_b = lax.psum_scatter(
        part_b.reshape(2, row_count // 2, ff - half_ff), "core", scatter_dimension=0, tiled=True
    ).reshape(N_DP // 2, rows_dev, ff - half_ff)
    part_a, part_b = lax.optimization_barrier((part_a, part_b))
    grad_a = lax.psum_scatter(part_a, DP, scatter_dimension=0, tiled=True)
    pieces = lax.all_to_all(part_b, CHIPS, split_axis=0, concat_axis=0, tiled=True)
    hidden_grad = jnp.concatenate([grad_a, jnp.sum(pieces, axis=0)], axis=1)

    up_grad = (hidden_grad * silu_vals * row_mask).astype(jnp.bfloat16)
    gate_grad = (
        hidden_grad * up_vals * sigmoid * (1.0 + gate_vals * (1.0 - sigmoid)) * row_mask
    ).astype(jnp.bfloat16)
    packed = jnp.stack([gate_grad, up_grad], axis=1)
    packed = lax.all_gather(packed, DP, axis=0, tiled=True)
    gate_g, up_g = packed[:, 0], packed[:, 1]

    down_terms = []
    gate_terms = []
    up_terms = []
    for which in range(expert_count):
        down_terms.append(contract_rows(hid_g * masks[which], dy_cols))
        gate_masked = gate_g * masks[which]
        up_masked = up_g * masks[which]
        gate_terms.append(contract_rows(x_cols, gate_masked))
        up_terms.append(contract_rows(x_cols, up_masked))
    down_total = jnp.stack(down_terms, 0)
    gate_total = jnp.stack(gate_terms, 0)
    up_total = jnp.stack(up_terms, 0)

    width = w_gate.shape[1]
    half_rows = row_count // 2
    summed = []
    for half in range(2):
        rows = slice(half * half_rows, (half + 1) * half_rows)
        partial_rows = jnp.zeros((half_rows, width), jnp.float32)
        for which in range(expert_count):
            gate_masked = gate_g[rows] * masks[which][rows]
            up_masked = up_g[rows] * masks[which][rows]
            partial_rows = (
                partial_rows
                + contract_cols(gate_masked, w_gate[which])
                + contract_cols(up_masked, w_up[which])
            )
        pieces = lax.all_to_all(
            partial_rows.reshape(N_TP, rows_dev, width), TP, split_axis=0, concat_axis=0, tiled=True
        )
        summed.append(jnp.sum(pieces, axis=0))
    summed = jnp.stack(summed, 0)
    core = lax.axis_index("core")
    low = lax.axis_index("x") < 2
    got = []
    for k in range(2):
        piece = lax.dynamic_index_in_dim(summed, core ^ k, 0, keepdims=False)
        got.append(lax.ppermute(piece, AXES, deliver_perm(k)))
    first = jnp.where(low, got[0], got[1])
    second = jnp.where(low, got[1], got[0])
    input_grad = jnp.concatenate([first, second], axis=1).astype(jnp.bfloat16)
    return (
        input_grad,
        gate_total.astype(jnp.bfloat16),
        up_total.astype(jnp.bfloat16),
        down_total.astype(jnp.bfloat16),
    )


def solution(mesh):
    fine = Mesh(mesh.devices.reshape(SIZES), AXES)
    return jax.shard_map(
        shards,
        mesh=fine,
        in_specs=(
            P(DP, None),
            P(DP, None),
            P(DP, TP),
            P(DP, TP),
            P(None, DP, TP),
            P(None, DP, TP),
            P(None, TP, DP),
            P(DP),
            P(),
        ),
        out_specs=(
            P(DP, TP),
            P(None, DP, TP),
            P(None, DP, TP),
            P(None, TP, DP),
        ),
        check_vma=False,
    )
```

```python
import numpy as np
import jax
import jax.numpy as jnp
from jax import lax
from jax.sharding import Mesh
from jax.sharding import PartitionSpec as P

BLOCK = 128
AXES = ("x", "ylo", "core", "z", "yhi")
SIZES = (4, 2, 2, 4, 2)
DP = ("x", "ylo", "core")
TP = ("z", "yhi")
CHIPS = ("x", "ylo")
N_DP = 16
N_TP = 8


def rank_of_pos(pos):
    core, x, ylo = pos // 8, (pos % 8) // 2, pos % 2
    return x * 4 + ylo * 2 + core


POS_RANK = np.array([rank_of_pos(p) for p in range(N_DP)], np.int32)


def deliver_perm(k):
    pairs = []
    for i in range(N_DP):
        for t in range(N_TP):
            dest = 8 * ((i % 2) ^ k) + t
            pairs.append((i * N_TP + t, dest * N_TP + i // 2))
    return pairs


def contract_rows(left_op, right_op):
    return lax.dot_general(
        left_op, right_op, (((0,), (0,)), ((), ())), preferred_element_type=jnp.float32
    )


def contract_cols(left_op, right_op):
    return lax.dot_general(
        left_op, right_op, (((1,), (1,)), ((), ())), preferred_element_type=jnp.float32
    )


def expert_masks(block_expert, row_count, expert_count):
    spread = jnp.broadcast_to(block_expert[:, None], (row_count // BLOCK, BLOCK)).reshape(
        row_count, 1
    )
    return [(spread == which).astype(jnp.bfloat16) for which in range(expert_count)]


def to_gathered_order(cols):
    width = cols.shape[1]
    return cols.reshape(4, 2, 2, BLOCK, width).transpose(2, 0, 1, 3, 4).reshape(-1, width)


def shards(rows_in, out_grad, gate_pre, up_pre, w_gate, w_up, w_down, live_rows, block_expert):
    rows_dev = rows_in.shape[0]
    expert_count = w_gate.shape[0]
    ff = gate_pre.shape[1]
    dy_cols = lax.all_to_all(out_grad, DP, split_axis=1, concat_axis=0, tiled=True)
    x_cols = lax.all_to_all(rows_in, DP, split_axis=1, concat_axis=0, tiled=True)
    x_cols, dy_cols = lax.optimization_barrier((x_cols, dy_cols))
    row_count = dy_cols.shape[0]
    expert_g = jnp.take(block_expert, jnp.asarray(POS_RANK), axis=0)
    masks_g = expert_masks(expert_g, row_count, expert_count)
    masks = expert_masks(block_expert, row_count, expert_count)

    positions = jnp.arange(rows_dev, dtype=jnp.int32)[:, None]
    row_mask = (positions < live_rows[0]).astype(jnp.float32)
    gate_vals = gate_pre.astype(jnp.float32)
    up_vals = up_pre.astype(jnp.float32)
    sigmoid = jax.nn.sigmoid(gate_vals)
    silu_vals = gate_vals * sigmoid
    hidden = (silu_vals * up_vals * row_mask).astype(jnp.bfloat16)

    dy_g = to_gathered_order(dy_cols)
    result = jnp.zeros((row_count, ff), jnp.float32)
    for which in range(expert_count):
        result = result + contract_cols(dy_g * masks_g[which], w_down[which])
    result = lax.psum_scatter(
        result.reshape(2, row_count // 2, ff), "core", scatter_dimension=0, tiled=True
    ).reshape(N_DP // 2, rows_dev, ff)
    hidden, result = lax.optimization_barrier((hidden, result))
    hid_g = lax.all_gather(hidden, DP, axis=0, tiled=True)
    pieces = lax.all_to_all(result, CHIPS, split_axis=0, concat_axis=0, tiled=True)
    hidden_grad = jnp.sum(pieces, axis=0)

    up_grad = (hidden_grad * silu_vals * row_mask).astype(jnp.bfloat16)
    gate_grad = (
        hidden_grad * up_vals * sigmoid * (1.0 + gate_vals * (1.0 - sigmoid)) * row_mask
    ).astype(jnp.bfloat16)
    packed = jnp.stack([gate_grad, up_grad], axis=1)
    packed = lax.all_gather(packed, DP, axis=0, tiled=True)
    gate_g, up_g = packed[:, 0], packed[:, 1]

    down_terms = []
    gate_terms = []
    up_terms = []
    for which in range(expert_count):
        down_terms.append(contract_rows(hid_g * masks[which], dy_cols))
        gate_masked = gate_g * masks[which]
        up_masked = up_g * masks[which]
        gate_terms.append(contract_rows(x_cols, gate_masked))
        up_terms.append(contract_rows(x_cols, up_masked))
    down_total = jnp.stack(down_terms, 0)
    gate_total = jnp.stack(gate_terms, 0)
    up_total = jnp.stack(up_terms, 0)

    width = w_gate.shape[1]
    half_rows = row_count // 2
    summed = []
    for half in range(2):
        rows = slice(half * half_rows, (half + 1) * half_rows)
        partial_rows = jnp.zeros((half_rows, width), jnp.float32)
        for which in range(expert_count):
            gate_masked = gate_g[rows] * masks[which][rows]
            up_masked = up_g[rows] * masks[which][rows]
            partial_rows = (
                partial_rows
                + contract_cols(gate_masked, w_gate[which])
                + contract_cols(up_masked, w_up[which])
            )
        pieces = lax.all_to_all(
            partial_rows.reshape(N_TP, rows_dev, width), TP, split_axis=0, concat_axis=0, tiled=True
        )
        summed.append(jnp.sum(pieces, axis=0))
    summed = jnp.stack(summed, 0)
    core = lax.axis_index("core")
    low = lax.axis_index("x") < 2
    got = []
    for k in range(2):
        piece = lax.dynamic_index_in_dim(summed, core ^ k, 0, keepdims=False)
        got.append(lax.ppermute(piece, AXES, deliver_perm(k)))
    first = jnp.where(low, got[0], got[1])
    second = jnp.where(low, got[1], got[0])
    input_grad = jnp.concatenate([first, second], axis=1).astype(jnp.bfloat16)
    return (
        input_grad,
        gate_total.astype(jnp.bfloat16),
        up_total.astype(jnp.bfloat16),
        down_total.astype(jnp.bfloat16),
    )


def solution(mesh):
    fine = Mesh(mesh.devices.reshape(SIZES), AXES)
    return jax.shard_map(
        shards,
        mesh=fine,
        in_specs=(
            P(DP, None),
            P(DP, None),
            P(DP, TP),
            P(DP, TP),
            P(None, DP, TP),
            P(None, DP, TP),
            P(None, TP, DP),
            P(DP),
            P(),
        ),
        out_specs=(
            P(DP, TP),
            P(None, DP, TP),
            P(None, DP, TP),
            P(None, TP, DP),
        ),
        check_vma=False,
    )
```

```python
import numpy as np
import jax
import jax.numpy as jnp
from jax import lax
from jax.sharding import Mesh
from jax.sharding import PartitionSpec as P

BLOCK = 128
AXES = ("x", "ylo", "core", "z", "yhi")
SIZES = (4, 2, 2, 4, 2)
DP = ("x", "ylo", "core")
TP = ("z", "yhi")
CHIPS = ("x", "ylo")
N_DP = 16
N_TP = 8


def rank_of_pos(pos):
    core, x, ylo = pos // 8, (pos % 8) // 2, pos % 2
    return x * 4 + ylo * 2 + core


POS_RANK = np.array([rank_of_pos(p) for p in range(N_DP)], np.int32)


def deliver_perm(k):
    pairs = []
    for i in range(N_DP):
        for t in range(N_TP):
            dest = 8 * ((i % 2) ^ k) + t
            pairs.append((i * N_TP + t, dest * N_TP + i // 2))
    return pairs


def contract_rows(left_op, right_op):
    return lax.dot_general(
        left_op, right_op, (((0,), (0,)), ((), ())), preferred_element_type=jnp.float32
    )


def contract_cols(left_op, right_op):
    return lax.dot_general(
        left_op, right_op, (((1,), (1,)), ((), ())), preferred_element_type=jnp.float32
    )


def expert_masks(block_expert, row_count, expert_count):
    spread = jnp.broadcast_to(block_expert[:, None], (row_count // BLOCK, BLOCK)).reshape(
        row_count, 1
    )
    return [(spread == which).astype(jnp.bfloat16) for which in range(expert_count)]


def to_gathered_order(cols):
    width = cols.shape[1]
    return cols.reshape(4, 2, 2, BLOCK, width).transpose(2, 0, 1, 3, 4).reshape(-1, width)


def shards(rows_in, out_grad, gate_pre, up_pre, w_gate, w_up, w_down, live_rows, block_expert):
    rows_dev = rows_in.shape[0]
    expert_count = w_gate.shape[0]
    ff = gate_pre.shape[1]
    dy_cols = lax.all_to_all(out_grad, DP, split_axis=1, concat_axis=0, tiled=True)
    row_count = dy_cols.shape[0]
    expert_g = jnp.take(block_expert, jnp.asarray(POS_RANK), axis=0)
    masks_g = expert_masks(expert_g, row_count, expert_count)
    masks = expert_masks(block_expert, row_count, expert_count)

    positions = jnp.arange(rows_dev, dtype=jnp.int32)[:, None]
    row_mask = (positions < live_rows[0]).astype(jnp.float32)
    gate_vals = gate_pre.astype(jnp.float32)
    up_vals = up_pre.astype(jnp.float32)
    sigmoid = jax.nn.sigmoid(gate_vals)
    silu_vals = gate_vals * sigmoid
    hidden = (silu_vals * up_vals * row_mask).astype(jnp.bfloat16)

    dy_g = to_gathered_order(dy_cols)
    result = jnp.zeros((row_count, ff), jnp.float32)
    for which in range(expert_count):
        result = result + contract_cols(dy_g * masks_g[which], w_down[which])
    result = lax.psum_scatter(
        result.reshape(2, row_count // 2, ff), "core", scatter_dimension=0, tiled=True
    ).reshape(N_DP // 2, rows_dev, ff)
    hidden, result = lax.optimization_barrier((hidden, result))
    hid_g = lax.all_gather(hidden, DP, axis=0, tiled=True)
    pieces = lax.all_to_all(result, CHIPS, split_axis=0, concat_axis=0, tiled=True)
    hidden_grad = jnp.sum(pieces, axis=0)
    rows_in, hidden_grad = lax.optimization_barrier((rows_in, hidden_grad))
    x_cols = lax.all_to_all(rows_in, DP, split_axis=1, concat_axis=0, tiled=True)

    up_grad = (hidden_grad * silu_vals * row_mask).astype(jnp.bfloat16)
    gate_grad = (
        hidden_grad * up_vals * sigmoid * (1.0 + gate_vals * (1.0 - sigmoid)) * row_mask
    ).astype(jnp.bfloat16)
    packed = jnp.stack([gate_grad, up_grad], axis=1)
    packed = lax.all_gather(packed, DP, axis=0, tiled=True)
    gate_g, up_g = packed[:, 0], packed[:, 1]

    down_terms = []
    gate_terms = []
    up_terms = []
    for which in range(expert_count):
        down_terms.append(contract_rows(hid_g * masks[which], dy_cols))
        gate_masked = gate_g * masks[which]
        up_masked = up_g * masks[which]
        gate_terms.append(contract_rows(x_cols, gate_masked))
        up_terms.append(contract_rows(x_cols, up_masked))
    down_total = jnp.stack(down_terms, 0)
    gate_total = jnp.stack(gate_terms, 0)
    up_total = jnp.stack(up_terms, 0)

    width = w_gate.shape[1]
    half_rows = row_count // 2
    summed = []
    for half in range(2):
        rows = slice(half * half_rows, (half + 1) * half_rows)
        partial_rows = jnp.zeros((half_rows, width), jnp.float32)
        for which in range(expert_count):
            gate_masked = gate_g[rows] * masks[which][rows]
            up_masked = up_g[rows] * masks[which][rows]
            partial_rows = (
                partial_rows
                + contract_cols(gate_masked, w_gate[which])
                + contract_cols(up_masked, w_up[which])
            )
        pieces = lax.all_to_all(
            partial_rows.reshape(N_TP, rows_dev, width), TP, split_axis=0, concat_axis=0, tiled=True
        )
        summed.append(jnp.sum(pieces, axis=0))
    summed = jnp.stack(summed, 0)
    core = lax.axis_index("core")
    low = lax.axis_index("x") < 2
    got = []
    for k in range(2):
        piece = lax.dynamic_index_in_dim(summed, core ^ k, 0, keepdims=False)
        got.append(lax.ppermute(piece, AXES, deliver_perm(k)))
    first = jnp.where(low, got[0], got[1])
    second = jnp.where(low, got[1], got[0])
    input_grad = jnp.concatenate([first, second], axis=1).astype(jnp.bfloat16)
    return (
        input_grad,
        gate_total.astype(jnp.bfloat16),
        up_total.astype(jnp.bfloat16),
        down_total.astype(jnp.bfloat16),
    )


def solution(mesh):
    fine = Mesh(mesh.devices.reshape(SIZES), AXES)
    return jax.shard_map(
        shards,
        mesh=fine,
        in_specs=(
            P(DP, None),
            P(DP, None),
            P(DP, TP),
            P(DP, TP),
            P(None, DP, TP),
            P(None, DP, TP),
            P(None, TP, DP),
            P(DP),
            P(),
        ),
        out_specs=(
            P(DP, TP),
            P(None, DP, TP),
            P(None, DP, TP),
            P(None, TP, DP),
        ),
        check_vma=False,
    )
```

```python
import numpy as np
import jax
import jax.numpy as jnp
from jax import lax
from jax.sharding import Mesh
from jax.sharding import PartitionSpec as P

BLOCK = 128
AXES = ("x", "ylo", "core", "z", "yhi")
SIZES = (4, 2, 2, 4, 2)
DP = ("x", "ylo", "core")
TP = ("z", "yhi")
CHIPS = ("x", "ylo")
N_DP = 16
N_TP = 8


def rank_of_pos(pos):
    core, x, ylo = pos // 8, (pos % 8) // 2, pos % 2
    return x * 4 + ylo * 2 + core


POS_RANK = np.array([rank_of_pos(p) for p in range(N_DP)], np.int32)


def deliver_perm(k):
    pairs = []
    for i in range(N_DP):
        for t in range(N_TP):
            dest = 8 * ((i % 2) ^ k) + t
            pairs.append((i * N_TP + t, dest * N_TP + i // 2))
    return pairs


def contract_rows(left_op, right_op):
    return lax.dot_general(
        left_op, right_op, (((0,), (0,)), ((), ())), preferred_element_type=jnp.float32
    )


def contract_cols(left_op, right_op):
    return lax.dot_general(
        left_op, right_op, (((1,), (1,)), ((), ())), preferred_element_type=jnp.float32
    )


def expert_masks(block_expert, row_count, expert_count):
    spread = jnp.broadcast_to(block_expert[:, None], (row_count // BLOCK, BLOCK)).reshape(
        row_count, 1
    )
    return [(spread == which).astype(jnp.bfloat16) for which in range(expert_count)]


def to_gathered_order(cols):
    width = cols.shape[1]
    return cols.reshape(4, 2, 2, BLOCK, width).transpose(2, 0, 1, 3, 4).reshape(-1, width)


def shards(rows_in, out_grad, gate_pre, up_pre, w_gate, w_up, w_down, live_rows, block_expert):
    rows_dev = rows_in.shape[0]
    expert_count = w_gate.shape[0]
    ff = gate_pre.shape[1]
    dy_cols = lax.all_to_all(out_grad, DP, split_axis=1, concat_axis=0, tiled=True)
    row_count = dy_cols.shape[0]
    expert_g = jnp.take(block_expert, jnp.asarray(POS_RANK), axis=0)
    masks_g = expert_masks(expert_g, row_count, expert_count)
    masks = expert_masks(block_expert, row_count, expert_count)

    positions = jnp.arange(rows_dev, dtype=jnp.int32)[:, None]
    row_mask = (positions < live_rows[0]).astype(jnp.float32)
    gate_vals = gate_pre.astype(jnp.float32)
    up_vals = up_pre.astype(jnp.float32)
    sigmoid = jax.nn.sigmoid(gate_vals)
    silu_vals = gate_vals * sigmoid
    hidden = (silu_vals * up_vals * row_mask).astype(jnp.bfloat16)

    dy_g = to_gathered_order(dy_cols)
    result = jnp.zeros((row_count, ff), jnp.float32)
    for which in range(expert_count):
        result = result + contract_cols(dy_g * masks_g[which], w_down[which])
    result = lax.psum_scatter(
        result.reshape(2, row_count // 2, ff), "core", scatter_dimension=0, tiled=True
    ).reshape(N_DP // 2, rows_dev, ff)
    hidden, result = lax.optimization_barrier((hidden, result))
    hid_g = lax.all_gather(hidden, DP, axis=0, tiled=True)
    pieces = lax.all_to_all(result, CHIPS, split_axis=0, concat_axis=0, tiled=True)
    hidden_grad = jnp.sum(pieces, axis=0)
    rows_in, hidden_grad = lax.optimization_barrier((rows_in, hidden_grad))
    x_cols = lax.all_to_all(rows_in, DP, split_axis=1, concat_axis=0, tiled=True)

    up_grad = (hidden_grad * silu_vals * row_mask).astype(jnp.bfloat16)
    gate_grad = (
        hidden_grad * up_vals * sigmoid * (1.0 + gate_vals * (1.0 - sigmoid)) * row_mask
    ).astype(jnp.bfloat16)
    gate_g = lax.all_gather(gate_grad, DP, axis=0, tiled=True)
    gate_g, up_grad = lax.optimization_barrier((gate_g, up_grad))
    up_g = lax.all_gather(up_grad, DP, axis=0, tiled=True)

    down_terms = []
    gate_terms = []
    up_terms = []
    for which in range(expert_count):
        down_terms.append(contract_rows(hid_g * masks[which], dy_cols))
        gate_masked = gate_g * masks[which]
        up_masked = up_g * masks[which]
        gate_terms.append(contract_rows(x_cols, gate_masked))
        up_terms.append(contract_rows(x_cols, up_masked))
    down_total = jnp.stack(down_terms, 0)
    gate_total = jnp.stack(gate_terms, 0)
    up_total = jnp.stack(up_terms, 0)

    width = w_gate.shape[1]
    half_rows = row_count // 2
    summed = []
    for half in range(2):
        rows = slice(half * half_rows, (half + 1) * half_rows)
        partial_rows = jnp.zeros((half_rows, width), jnp.float32)
        for which in range(expert_count):
            gate_masked = gate_g[rows] * masks[which][rows]
            up_masked = up_g[rows] * masks[which][rows]
            partial_rows = (
                partial_rows
                + contract_cols(gate_masked, w_gate[which])
                + contract_cols(up_masked, w_up[which])
            )
        pieces = lax.all_to_all(
            partial_rows.reshape(N_TP, rows_dev, width), TP, split_axis=0, concat_axis=0, tiled=True
        )
        summed.append(jnp.sum(pieces, axis=0))
    summed = jnp.stack(summed, 0)
    core = lax.axis_index("core")
    low = lax.axis_index("x") < 2
    got = []
    for k in range(2):
        piece = lax.dynamic_index_in_dim(summed, core ^ k, 0, keepdims=False)
        got.append(lax.ppermute(piece, AXES, deliver_perm(k)))
    first = jnp.where(low, got[0], got[1])
    second = jnp.where(low, got[1], got[0])
    input_grad = jnp.concatenate([first, second], axis=1).astype(jnp.bfloat16)
    return (
        input_grad,
        gate_total.astype(jnp.bfloat16),
        up_total.astype(jnp.bfloat16),
        down_total.astype(jnp.bfloat16),
    )


def solution(mesh):
    fine = Mesh(mesh.devices.reshape(SIZES), AXES)
    return jax.shard_map(
        shards,
        mesh=fine,
        in_specs=(
            P(DP, None),
            P(DP, None),
            P(DP, TP),
            P(DP, TP),
            P(None, DP, TP),
            P(None, DP, TP),
            P(None, TP, DP),
            P(DP),
            P(),
        ),
        out_specs=(
            P(DP, TP),
            P(None, DP, TP),
            P(None, DP, TP),
            P(None, TP, DP),
        ),
        check_vma=False,
    )
```

```python
import numpy as np
import jax
import jax.numpy as jnp
from jax import lax
from jax.sharding import Mesh
from jax.sharding import PartitionSpec as P

BLOCK = 128
AXES = ("x", "ylo", "core", "z", "yhi")
SIZES = (4, 2, 2, 4, 2)
DP = ("x", "ylo", "core")
TP = ("z", "yhi")
CHIPS = ("x", "ylo")
N_DP = 16
N_TP = 8


def rank_of_pos(pos):
    core, x, ylo = pos // 8, (pos % 8) // 2, pos % 2
    return x * 4 + ylo * 2 + core


POS_RANK = np.array([rank_of_pos(p) for p in range(N_DP)], np.int32)


def deliver_perm(k):
    pairs = []
    for i in range(N_DP):
        for t in range(N_TP):
            dest = 8 * ((i % 2) ^ k) + t
            pairs.append((i * N_TP + t, dest * N_TP + i // 2))
    return pairs


def contract_rows(left_op, right_op):
    return lax.dot_general(
        left_op, right_op, (((0,), (0,)), ((), ())), preferred_element_type=jnp.float32
    )


def contract_cols(left_op, right_op):
    return lax.dot_general(
        left_op, right_op, (((1,), (1,)), ((), ())), preferred_element_type=jnp.float32
    )


def expert_masks(block_expert, row_count, expert_count):
    spread = jnp.broadcast_to(block_expert[:, None], (row_count // BLOCK, BLOCK)).reshape(
        row_count, 1
    )
    return [(spread == which).astype(jnp.bfloat16) for which in range(expert_count)]


def to_gathered_order(cols):
    width = cols.shape[1]
    return cols.reshape(4, 2, 2, BLOCK, width).transpose(2, 0, 1, 3, 4).reshape(-1, width)


def shards(rows_in, out_grad, gate_pre, up_pre, w_gate, w_up, w_down, live_rows, block_expert):
    rows_dev = rows_in.shape[0]
    expert_count = w_gate.shape[0]
    ff = gate_pre.shape[1]
    dy_cols = lax.all_to_all(out_grad, DP, split_axis=1, concat_axis=0, tiled=True)
    row_count = dy_cols.shape[0]
    expert_g = jnp.take(block_expert, jnp.asarray(POS_RANK), axis=0)
    masks_g = expert_masks(expert_g, row_count, expert_count)
    masks = expert_masks(block_expert, row_count, expert_count)

    positions = jnp.arange(rows_dev, dtype=jnp.int32)[:, None]
    row_mask = (positions < live_rows[0]).astype(jnp.float32)
    gate_vals = gate_pre.astype(jnp.float32)
    up_vals = up_pre.astype(jnp.float32)
    sigmoid = jax.nn.sigmoid(gate_vals)
    silu_vals = gate_vals * sigmoid
    hidden = (silu_vals * up_vals * row_mask).astype(jnp.bfloat16)
    hid_g = lax.all_gather(hidden, DP, axis=0, tiled=True)

    dy_g = to_gathered_order(dy_cols)
    result = jnp.zeros((row_count, ff), jnp.float32)
    for which in range(expert_count):
        result = result + contract_cols(dy_g * masks_g[which], w_down[which])
    hid_g, result = lax.optimization_barrier((hid_g, result))
    result = lax.psum_scatter(
        result.reshape(2, row_count // 2, ff), "core", scatter_dimension=0, tiled=True
    ).reshape(N_DP // 2, rows_dev, ff)
    pieces = lax.all_to_all(result, CHIPS, split_axis=0, concat_axis=0, tiled=True)
    hidden_grad = jnp.sum(pieces, axis=0)
    rows_in, hidden_grad = lax.optimization_barrier((rows_in, hidden_grad))
    x_cols = lax.all_to_all(rows_in, DP, split_axis=1, concat_axis=0, tiled=True)

    up_grad = (hidden_grad * silu_vals * row_mask).astype(jnp.bfloat16)
    gate_grad = (
        hidden_grad * up_vals * sigmoid * (1.0 + gate_vals * (1.0 - sigmoid)) * row_mask
    ).astype(jnp.bfloat16)
    packed = jnp.stack([gate_grad, up_grad], axis=1)
    packed = lax.all_gather(packed, DP, axis=0, tiled=True)
    gate_g, up_g = packed[:, 0], packed[:, 1]

    down_terms = []
    gate_terms = []
    up_terms = []
    for which in range(expert_count):
        down_terms.append(contract_rows(hid_g * masks[which], dy_cols))
        gate_masked = gate_g * masks[which]
        up_masked = up_g * masks[which]
        gate_terms.append(contract_rows(x_cols, gate_masked))
        up_terms.append(contract_rows(x_cols, up_masked))
    down_total = jnp.stack(down_terms, 0)
    gate_total = jnp.stack(gate_terms, 0)
    up_total = jnp.stack(up_terms, 0)

    width = w_gate.shape[1]
    half_rows = row_count // 2
    summed = []
    for half in range(2):
        rows = slice(half * half_rows, (half + 1) * half_rows)
        partial_rows = jnp.zeros((half_rows, width), jnp.float32)
        for which in range(expert_count):
            gate_masked = gate_g[rows] * masks[which][rows]
            up_masked = up_g[rows] * masks[which][rows]
            partial_rows = (
                partial_rows
                + contract_cols(gate_masked, w_gate[which])
                + contract_cols(up_masked, w_up[which])
            )
        pieces = lax.all_to_all(
            partial_rows.reshape(N_TP, rows_dev, width), TP, split_axis=0, concat_axis=0, tiled=True
        )
        summed.append(jnp.sum(pieces, axis=0))
    summed = jnp.stack(summed, 0)
    core = lax.axis_index("core")
    low = lax.axis_index("x") < 2
    got = []
    for k in range(2):
        piece = lax.dynamic_index_in_dim(summed, core ^ k, 0, keepdims=False)
        got.append(lax.ppermute(piece, AXES, deliver_perm(k)))
    first = jnp.where(low, got[0], got[1])
    second = jnp.where(low, got[1], got[0])
    input_grad = jnp.concatenate([first, second], axis=1).astype(jnp.bfloat16)
    return (
        input_grad,
        gate_total.astype(jnp.bfloat16),
        up_total.astype(jnp.bfloat16),
        down_total.astype(jnp.bfloat16),
    )


def solution(mesh):
    fine = Mesh(mesh.devices.reshape(SIZES), AXES)
    return jax.shard_map(
        shards,
        mesh=fine,
        in_specs=(
            P(DP, None),
            P(DP, None),
            P(DP, TP),
            P(DP, TP),
            P(None, DP, TP),
            P(None, DP, TP),
            P(None, TP, DP),
            P(DP),
            P(),
        ),
        out_specs=(
            P(DP, TP),
            P(None, DP, TP),
            P(None, DP, TP),
            P(None, TP, DP),
        ),
        check_vma=False,
    )
```

```python
import numpy as np
import jax
import jax.numpy as jnp
from jax import lax
from jax.sharding import Mesh
from jax.sharding import PartitionSpec as P

BLOCK = 128
AXES = ("x", "ylo", "core", "z", "yhi")
SIZES = (4, 2, 2, 4, 2)
DP = ("x", "ylo", "core")
TP = ("z", "yhi")
CHIPS = ("x", "ylo")
N_DP = 16
N_TP = 8


def rank_of_pos(pos):
    core, x, ylo = pos // 8, (pos % 8) // 2, pos % 2
    return x * 4 + ylo * 2 + core


POS_RANK = np.array([rank_of_pos(p) for p in range(N_DP)], np.int32)


def deliver_perm(k):
    pairs = []
    for i in range(N_DP):
        for t in range(N_TP):
            dest = 8 * ((i % 2) ^ k) + t
            pairs.append((i * N_TP + t, dest * N_TP + i // 2))
    return pairs


def contract_rows(left_op, right_op):
    return lax.dot_general(
        left_op, right_op, (((0,), (0,)), ((), ())), preferred_element_type=jnp.float32
    )


def contract_cols(left_op, right_op):
    return lax.dot_general(
        left_op, right_op, (((1,), (1,)), ((), ())), preferred_element_type=jnp.float32
    )


def expert_masks(block_expert, row_count, expert_count):
    spread = jnp.broadcast_to(block_expert[:, None], (row_count // BLOCK, BLOCK)).reshape(
        row_count, 1
    )
    return [(spread == which).astype(jnp.bfloat16) for which in range(expert_count)]


def to_gathered_order(cols):
    width = cols.shape[1]
    return cols.reshape(4, 2, 2, BLOCK, width).transpose(2, 0, 1, 3, 4).reshape(-1, width)


def shards(rows_in, out_grad, gate_pre, up_pre, w_gate, w_up, w_down, live_rows, block_expert):
    rows_dev = rows_in.shape[0]
    expert_count = w_gate.shape[0]
    ff = gate_pre.shape[1]
    dy_cols = lax.all_to_all(out_grad, DP, split_axis=1, concat_axis=0, tiled=True)
    row_count = dy_cols.shape[0]
    expert_g = jnp.take(block_expert, jnp.asarray(POS_RANK), axis=0)
    masks_g = expert_masks(expert_g, row_count, expert_count)
    masks = expert_masks(block_expert, row_count, expert_count)

    positions = jnp.arange(rows_dev, dtype=jnp.int32)[:, None]
    row_mask = (positions < live_rows[0]).astype(jnp.float32)
    gate_vals = gate_pre.astype(jnp.float32)
    up_vals = up_pre.astype(jnp.float32)
    sigmoid = jax.nn.sigmoid(gate_vals)
    silu_vals = gate_vals * sigmoid
    hidden = (silu_vals * up_vals * row_mask).astype(jnp.bfloat16)
    hid_g = lax.all_gather(hidden, DP, axis=0, tiled=True)

    dy_g = to_gathered_order(dy_cols)
    result = jnp.zeros((row_count, ff), jnp.float32)
    for which in range(expert_count):
        result = result + contract_cols(dy_g * masks_g[which], w_down[which])
    hid_g, result = lax.optimization_barrier((hid_g, result))
    result = lax.psum_scatter(
        result.reshape(2, row_count // 2, ff), "core", scatter_dimension=0, tiled=True
    ).reshape(N_DP // 2, rows_dev, ff)
    pieces = lax.all_to_all(result, CHIPS, split_axis=0, concat_axis=0, tiled=True)
    hidden_grad = jnp.sum(pieces, axis=0)
    rows_in, hidden_grad = lax.optimization_barrier((rows_in, hidden_grad))
    x_cols = lax.all_to_all(rows_in, DP, split_axis=1, concat_axis=0, tiled=True)

    up_grad = (hidden_grad * silu_vals * row_mask).astype(jnp.bfloat16)
    gate_grad = (
        hidden_grad * up_vals * sigmoid * (1.0 + gate_vals * (1.0 - sigmoid)) * row_mask
    ).astype(jnp.bfloat16)
    gate_g = lax.all_gather(gate_grad, DP, axis=0, tiled=True)
    up_g = lax.all_gather(up_grad, DP, axis=0, tiled=True)

    down_terms = []
    gate_terms = []
    up_terms = []
    for which in range(expert_count):
        down_terms.append(contract_rows(hid_g * masks[which], dy_cols))
        gate_masked = gate_g * masks[which]
        up_masked = up_g * masks[which]
        gate_terms.append(contract_rows(x_cols, gate_masked))
        up_terms.append(contract_rows(x_cols, up_masked))
    down_total = jnp.stack(down_terms, 0)
    gate_total = jnp.stack(gate_terms, 0)
    up_total = jnp.stack(up_terms, 0)

    width = w_gate.shape[1]
    half_rows = row_count // 2
    summed = []
    for half in range(2):
        rows = slice(half * half_rows, (half + 1) * half_rows)
        partial_rows = jnp.zeros((half_rows, width), jnp.float32)
        for which in range(expert_count):
            gate_masked = gate_g[rows] * masks[which][rows]
            up_masked = up_g[rows] * masks[which][rows]
            partial_rows = (
                partial_rows
                + contract_cols(gate_masked, w_gate[which])
                + contract_cols(up_masked, w_up[which])
            )
        pieces = lax.all_to_all(
            partial_rows.reshape(N_TP, rows_dev, width), TP, split_axis=0, concat_axis=0, tiled=True
        )
        summed.append(jnp.sum(pieces, axis=0))
    summed = jnp.stack(summed, 0)
    core = lax.axis_index("core")
    low = lax.axis_index("x") < 2
    got = []
    for k in range(2):
        piece = lax.dynamic_index_in_dim(summed, core ^ k, 0, keepdims=False)
        got.append(lax.ppermute(piece, AXES, deliver_perm(k)))
    first = jnp.where(low, got[0], got[1])
    second = jnp.where(low, got[1], got[0])
    input_grad = jnp.concatenate([first, second], axis=1).astype(jnp.bfloat16)
    return (
        input_grad,
        gate_total.astype(jnp.bfloat16),
        up_total.astype(jnp.bfloat16),
        down_total.astype(jnp.bfloat16),
    )


def solution(mesh):
    fine = Mesh(mesh.devices.reshape(SIZES), AXES)
    return jax.shard_map(
        shards,
        mesh=fine,
        in_specs=(
            P(DP, None),
            P(DP, None),
            P(DP, TP),
            P(DP, TP),
            P(None, DP, TP),
            P(None, DP, TP),
            P(None, TP, DP),
            P(DP),
            P(),
        ),
        out_specs=(
            P(DP, TP),
            P(None, DP, TP),
            P(None, DP, TP),
            P(None, TP, DP),
        ),
        check_vma=False,
    )
```

```python
import numpy as np
import jax
import jax.numpy as jnp
from jax import lax
from jax.sharding import Mesh
from jax.sharding import PartitionSpec as P

BLOCK = 128
AXES = ("x", "ylo", "core", "z", "yhi")
SIZES = (4, 2, 2, 4, 2)
DP = ("x", "ylo", "core")
TP = ("z", "yhi")
CHIPS = ("x", "ylo")
N_DP = 16
N_TP = 8


def rank_of_pos(pos):
    core, x, ylo = pos // 8, (pos % 8) // 2, pos % 2
    return x * 4 + ylo * 2 + core


POS_RANK = np.array([rank_of_pos(p) for p in range(N_DP)], np.int32)


def deliver_perm(k):
    pairs = []
    for i in range(N_DP):
        for t in range(N_TP):
            dest = 8 * ((i % 2) ^ k) + t
            pairs.append((i * N_TP + t, dest * N_TP + i // 2))
    return pairs


def contract_rows(left_op, right_op):
    return lax.dot_general(
        left_op, right_op, (((0,), (0,)), ((), ())), preferred_element_type=jnp.float32
    )


def contract_cols(left_op, right_op):
    return lax.dot_general(
        left_op, right_op, (((1,), (1,)), ((), ())), preferred_element_type=jnp.float32
    )


def expert_masks(block_expert, row_count, expert_count):
    spread = jnp.broadcast_to(block_expert[:, None], (row_count // BLOCK, BLOCK)).reshape(
        row_count, 1
    )
    return [(spread == which).astype(jnp.bfloat16) for which in range(expert_count)]


def to_gathered_order(cols):
    width = cols.shape[1]
    return cols.reshape(4, 2, 2, BLOCK, width).transpose(2, 0, 1, 3, 4).reshape(-1, width)


def shards(rows_in, out_grad, gate_pre, up_pre, w_gate, w_up, w_down, live_rows, block_expert):
    rows_dev = rows_in.shape[0]
    expert_count = w_gate.shape[0]
    ff = gate_pre.shape[1]
    dy_cols = lax.all_to_all(out_grad, DP, split_axis=1, concat_axis=0, tiled=True)
    row_count = dy_cols.shape[0]
    expert_g = jnp.take(block_expert, jnp.asarray(POS_RANK), axis=0)
    masks_g = expert_masks(expert_g, row_count, expert_count)
    masks = expert_masks(block_expert, row_count, expert_count)

    positions = jnp.arange(rows_dev, dtype=jnp.int32)[:, None]
    row_mask = (positions < live_rows[0]).astype(jnp.float32)
    gate_vals = gate_pre.astype(jnp.float32)
    up_vals = up_pre.astype(jnp.float32)
    sigmoid = jax.nn.sigmoid(gate_vals)
    silu_vals = gate_vals * sigmoid
    hidden = (silu_vals * up_vals * row_mask).astype(jnp.bfloat16)
    hid_g = lax.all_gather(hidden, DP, axis=0, tiled=True)

    dy_g = to_gathered_order(dy_cols)
    result = jnp.zeros((row_count, ff), jnp.float32)
    for which in range(expert_count):
        result = result + contract_cols(dy_g * masks_g[which], w_down[which])
    hid_g, result = lax.optimization_barrier((hid_g, result))
    cut = ff // 2
    halves = []
    for lo, hi in ((0, cut), (cut, ff)):
        halves.append(
            lax.psum_scatter(
                result[:, lo:hi].reshape(2, row_count // 2, hi - lo), "core", scatter_dimension=0, tiled=True
            ).reshape(N_DP // 2, rows_dev, hi - lo)
            if not halves
            else result[:, lo:hi]
        )
    first_half, rest = lax.optimization_barrier((halves[0], halves[1]))
    rest = lax.psum_scatter(
        rest.reshape(2, row_count // 2, ff - cut), "core", scatter_dimension=0, tiled=True
    ).reshape(N_DP // 2, rows_dev, ff - cut)
    hidden_grad = []
    for part in (first_half, rest):
        pieces = lax.all_to_all(part, CHIPS, split_axis=0, concat_axis=0, tiled=True)
        hidden_grad.append(jnp.sum(pieces, axis=0))
    hidden_grad = jnp.concatenate(hidden_grad, axis=1)
    rows_in, hidden_grad = lax.optimization_barrier((rows_in, hidden_grad))
    x_cols = lax.all_to_all(rows_in, DP, split_axis=1, concat_axis=0, tiled=True)

    up_grad = (hidden_grad * silu_vals * row_mask).astype(jnp.bfloat16)
    gate_grad = (
        hidden_grad * up_vals * sigmoid * (1.0 + gate_vals * (1.0 - sigmoid)) * row_mask
    ).astype(jnp.bfloat16)
    packed = jnp.stack([gate_grad, up_grad], axis=1)
    packed = lax.all_gather(packed, DP, axis=0, tiled=True)
    gate_g, up_g = packed[:, 0], packed[:, 1]

    down_terms = []
    gate_terms = []
    up_terms = []
    for which in range(expert_count):
        down_terms.append(contract_rows(hid_g * masks[which], dy_cols))
        gate_masked = gate_g * masks[which]
        up_masked = up_g * masks[which]
        gate_terms.append(contract_rows(x_cols, gate_masked))
        up_terms.append(contract_rows(x_cols, up_masked))
    down_total = jnp.stack(down_terms, 0)
    gate_total = jnp.stack(gate_terms, 0)
    up_total = jnp.stack(up_terms, 0)

    width = w_gate.shape[1]
    half_rows = row_count // 2
    summed = []
    for half in range(2):
        rows = slice(half * half_rows, (half + 1) * half_rows)
        partial_rows = jnp.zeros((half_rows, width), jnp.float32)
        for which in range(expert_count):
            gate_masked = gate_g[rows] * masks[which][rows]
            up_masked = up_g[rows] * masks[which][rows]
            partial_rows = (
                partial_rows
                + contract_cols(gate_masked, w_gate[which])
                + contract_cols(up_masked, w_up[which])
            )
        pieces = lax.all_to_all(
            partial_rows.reshape(N_TP, rows_dev, width), TP, split_axis=0, concat_axis=0, tiled=True
        )
        summed.append(jnp.sum(pieces, axis=0))
    summed = jnp.stack(summed, 0)
    core = lax.axis_index("core")
    low = lax.axis_index("x") < 2
    got = []
    for k in range(2):
        piece = lax.dynamic_index_in_dim(summed, core ^ k, 0, keepdims=False)
        got.append(lax.ppermute(piece, AXES, deliver_perm(k)))
    first = jnp.where(low, got[0], got[1])
    second = jnp.where(low, got[1], got[0])
    input_grad = jnp.concatenate([first, second], axis=1).astype(jnp.bfloat16)
    return (
        input_grad,
        gate_total.astype(jnp.bfloat16),
        up_total.astype(jnp.bfloat16),
        down_total.astype(jnp.bfloat16),
    )


def solution(mesh):
    fine = Mesh(mesh.devices.reshape(SIZES), AXES)
    return jax.shard_map(
        shards,
        mesh=fine,
        in_specs=(
            P(DP, None),
            P(DP, None),
            P(DP, TP),
            P(DP, TP),
            P(None, DP, TP),
            P(None, DP, TP),
            P(None, TP, DP),
            P(DP),
            P(),
        ),
        out_specs=(
            P(DP, TP),
            P(None, DP, TP),
            P(None, DP, TP),
            P(None, TP, DP),
        ),
        check_vma=False,
    )
```

```python
import numpy as np
import jax
import jax.numpy as jnp
from jax import lax
from jax.sharding import Mesh
from jax.sharding import PartitionSpec as P

BLOCK = 128
AXES = ("x", "ylo", "core", "z", "yhi")
SIZES = (4, 2, 2, 4, 2)
DP = ("x", "ylo", "core")
TP = ("z", "yhi")
CHIPS = ("x", "ylo")
N_DP = 16
N_TP = 8


def rank_of_pos(pos):
    core, x, ylo = pos // 8, (pos % 8) // 2, pos % 2
    return x * 4 + ylo * 2 + core


POS_RANK = np.array([rank_of_pos(p) for p in range(N_DP)], np.int32)


def deliver_perm(k):
    pairs = []
    for i in range(N_DP):
        for t in range(N_TP):
            dest = 8 * ((i % 2) ^ k) + t
            pairs.append((i * N_TP + t, dest * N_TP + i // 2))
    return pairs


def contract_rows(left_op, right_op):
    return lax.dot_general(
        left_op, right_op, (((0,), (0,)), ((), ())), preferred_element_type=jnp.float32
    )


def contract_cols(left_op, right_op):
    return lax.dot_general(
        left_op, right_op, (((1,), (1,)), ((), ())), preferred_element_type=jnp.float32
    )


def expert_masks(block_expert, row_count, expert_count):
    spread = jnp.broadcast_to(block_expert[:, None], (row_count // BLOCK, BLOCK)).reshape(
        row_count, 1
    )
    return [(spread == which).astype(jnp.bfloat16) for which in range(expert_count)]


def to_gathered_order(cols):
    width = cols.shape[1]
    return cols.reshape(4, 2, 2, BLOCK, width).transpose(2, 0, 1, 3, 4).reshape(-1, width)


def shards(rows_in, out_grad, gate_pre, up_pre, w_gate, w_up, w_down, live_rows, block_expert):
    rows_dev = rows_in.shape[0]
    expert_count = w_gate.shape[0]
    ff = gate_pre.shape[1]
    dy_cols = lax.all_to_all(out_grad, DP, split_axis=1, concat_axis=0, tiled=True)
    row_count = dy_cols.shape[0]
    expert_g = jnp.take(block_expert, jnp.asarray(POS_RANK), axis=0)
    masks_g = expert_masks(expert_g, row_count, expert_count)
    masks = expert_masks(block_expert, row_count, expert_count)

    positions = jnp.arange(rows_dev, dtype=jnp.int32)[:, None]
    row_mask = (positions < live_rows[0]).astype(jnp.float32)
    gate_vals = gate_pre.astype(jnp.float32)
    up_vals = up_pre.astype(jnp.float32)
    sigmoid = jax.nn.sigmoid(gate_vals)
    silu_vals = gate_vals * sigmoid
    hidden = (silu_vals * up_vals * row_mask).astype(jnp.bfloat16)
    hid_g = lax.all_gather(hidden, DP, axis=0, tiled=True)

    dy_g = to_gathered_order(dy_cols)
    result = jnp.zeros((row_count, ff), jnp.float32)
    for which in range(expert_count):
        result = result + contract_cols(dy_g * masks_g[which], w_down[which])
    hid_g, result = lax.optimization_barrier((hid_g, result))
    result = lax.psum_scatter(
        result.reshape(2, row_count // 2, ff), "core", scatter_dimension=0, tiled=True
    ).reshape(N_DP // 2, rows_dev, ff)
    pieces = lax.all_to_all(result, CHIPS, split_axis=0, concat_axis=0, tiled=True)
    hidden_grad = jnp.sum(pieces, axis=0)
    rows_in, hidden_grad = lax.optimization_barrier((rows_in, hidden_grad))
    x_cols = lax.all_to_all(rows_in, DP, split_axis=1, concat_axis=0, tiled=True)

    up_grad = (hidden_grad * silu_vals * row_mask).astype(jnp.bfloat16)
    gate_grad = (
        hidden_grad * up_vals * sigmoid * (1.0 + gate_vals * (1.0 - sigmoid)) * row_mask
    ).astype(jnp.bfloat16)
    packed = jnp.stack([gate_grad, up_grad], axis=1)
    packed = lax.all_gather(packed, DP, axis=0, tiled=True)
    gate_g, up_g = packed[:, 0], packed[:, 1]

    down_terms = []
    gate_terms = []
    up_terms = []
    for which in range(expert_count):
        gate_masked = gate_g * masks[which]
        up_masked = up_g * masks[which]
        gate_terms.append(contract_rows(x_cols, gate_masked))
        up_terms.append(contract_rows(x_cols, up_masked))
    gate_total = jnp.stack(gate_terms, 0)
    up_total = jnp.stack(up_terms, 0)

    width = w_gate.shape[1]
    half_rows = row_count // 2
    summed = []
    for half in range(2):
        rows = slice(half * half_rows, (half + 1) * half_rows)
        partial_rows = jnp.zeros((half_rows, width), jnp.float32)
        for which in range(expert_count):
            gate_masked = gate_g[rows] * masks[which][rows]
            up_masked = up_g[rows] * masks[which][rows]
            partial_rows = (
                partial_rows
                + contract_cols(gate_masked, w_gate[which])
                + contract_cols(up_masked, w_up[which])
            )
        pieces = lax.all_to_all(
            partial_rows.reshape(N_TP, rows_dev, width), TP, split_axis=0, concat_axis=0, tiled=True
        )
        summed.append(jnp.sum(pieces, axis=0))
    summed = jnp.stack(summed, 0)
    hid_g, summed = lax.optimization_barrier((hid_g, summed))
    for which in range(expert_count):
        down_terms.append(contract_rows(hid_g * masks[which], dy_cols))
    down_total = jnp.stack(down_terms, 0)
    core = lax.axis_index("core")
    low = lax.axis_index("x") < 2
    got = []
    for k in range(2):
        piece = lax.dynamic_index_in_dim(summed, core ^ k, 0, keepdims=False)
        got.append(lax.ppermute(piece, AXES, deliver_perm(k)))
    first = jnp.where(low, got[0], got[1])
    second = jnp.where(low, got[1], got[0])
    input_grad = jnp.concatenate([first, second], axis=1).astype(jnp.bfloat16)
    return (
        input_grad,
        gate_total.astype(jnp.bfloat16),
        up_total.astype(jnp.bfloat16),
        down_total.astype(jnp.bfloat16),
    )


def solution(mesh):
    fine = Mesh(mesh.devices.reshape(SIZES), AXES)
    return jax.shard_map(
        shards,
        mesh=fine,
        in_specs=(
            P(DP, None),
            P(DP, None),
            P(DP, TP),
            P(DP, TP),
            P(None, DP, TP),
            P(None, DP, TP),
            P(None, TP, DP),
            P(DP),
            P(),
        ),
        out_specs=(
            P(DP, TP),
            P(None, DP, TP),
            P(None, DP, TP),
            P(None, TP, DP),
        ),
        check_vma=False,
    )
```

```python
import numpy as np
import jax
import jax.numpy as jnp
from jax import lax
from jax.sharding import Mesh
from jax.sharding import PartitionSpec as P

BLOCK = 128
AXES = ("x", "ylo", "core", "z", "yhi")
SIZES = (4, 2, 2, 4, 2)
DP = ("x", "ylo", "core")
TP = ("z", "yhi")
CHIPS = ("x", "ylo")
N_DP = 16
N_TP = 8


def rank_of_pos(pos):
    core, x, ylo = pos // 8, (pos % 8) // 2, pos % 2
    return x * 4 + ylo * 2 + core


POS_RANK = np.array([rank_of_pos(p) for p in range(N_DP)], np.int32)


def deliver_perm(half, parity):
    pairs = []
    for i in range(parity, N_DP, 2):
        for t in range(N_TP):
            pairs.append((i * N_TP + t, (8 * half + t) * N_TP + i // 2))
    return pairs


def contract_rows(left_op, right_op):
    return lax.dot_general(
        left_op, right_op, (((0,), (0,)), ((), ())), preferred_element_type=jnp.float32
    )


def contract_cols(left_op, right_op):
    return lax.dot_general(
        left_op, right_op, (((1,), (1,)), ((), ())), preferred_element_type=jnp.float32
    )


def expert_masks(block_expert, row_count, expert_count):
    spread = jnp.broadcast_to(block_expert[:, None], (row_count // BLOCK, BLOCK)).reshape(
        row_count, 1
    )
    return [(spread == which).astype(jnp.bfloat16) for which in range(expert_count)]


def to_gathered_order(cols):
    width = cols.shape[1]
    return cols.reshape(4, 2, 2, BLOCK, width).transpose(2, 0, 1, 3, 4).reshape(-1, width)


def shards(rows_in, out_grad, gate_pre, up_pre, w_gate, w_up, w_down, live_rows, block_expert):
    rows_dev = rows_in.shape[0]
    expert_count = w_gate.shape[0]
    ff = gate_pre.shape[1]
    dy_cols = lax.all_to_all(out_grad, DP, split_axis=1, concat_axis=0, tiled=True)
    row_count = dy_cols.shape[0]
    expert_g = jnp.take(block_expert, jnp.asarray(POS_RANK), axis=0)
    masks_g = expert_masks(expert_g, row_count, expert_count)
    masks = expert_masks(block_expert, row_count, expert_count)

    positions = jnp.arange(rows_dev, dtype=jnp.int32)[:, None]
    row_mask = (positions < live_rows[0]).astype(jnp.float32)
    gate_vals = gate_pre.astype(jnp.float32)
    up_vals = up_pre.astype(jnp.float32)
    sigmoid = jax.nn.sigmoid(gate_vals)
    silu_vals = gate_vals * sigmoid
    hidden = (silu_vals * up_vals * row_mask).astype(jnp.bfloat16)
    hid_g = lax.all_gather(hidden, DP, axis=0, tiled=True)

    dy_g = to_gathered_order(dy_cols)
    result = jnp.zeros((row_count, ff), jnp.float32)
    for which in range(expert_count):
        result = result + contract_cols(dy_g * masks_g[which], w_down[which])
    hid_g, result = lax.optimization_barrier((hid_g, result))
    result = lax.psum_scatter(
        result.reshape(2, row_count // 2, ff), "core", scatter_dimension=0, tiled=True
    ).reshape(N_DP // 2, rows_dev, ff)
    pieces = lax.all_to_all(result, CHIPS, split_axis=0, concat_axis=0, tiled=True)
    hidden_grad = jnp.sum(pieces, axis=0)
    rows_in, hidden_grad = lax.optimization_barrier((rows_in, hidden_grad))
    x_cols = lax.all_to_all(rows_in, DP, split_axis=1, concat_axis=0, tiled=True)

    up_grad = (hidden_grad * silu_vals * row_mask).astype(jnp.bfloat16)
    gate_grad = (
        hidden_grad * up_vals * sigmoid * (1.0 + gate_vals * (1.0 - sigmoid)) * row_mask
    ).astype(jnp.bfloat16)
    packed = jnp.stack([gate_grad, up_grad], axis=1)
    packed = lax.all_gather(packed, DP, axis=0, tiled=True)
    gate_g, up_g = packed[:, 0], packed[:, 1]

    down_terms = []
    gate_terms = []
    up_terms = []
    for which in range(expert_count):
        down_terms.append(contract_rows(hid_g * masks[which], dy_cols))
        gate_masked = gate_g * masks[which]
        up_masked = up_g * masks[which]
        gate_terms.append(contract_rows(x_cols, gate_masked))
        up_terms.append(contract_rows(x_cols, up_masked))
    down_total = jnp.stack(down_terms, 0)
    gate_total = jnp.stack(gate_terms, 0)
    up_total = jnp.stack(up_terms, 0)

    width = w_gate.shape[1]
    half_rows = row_count // 2
    summed = []
    for half in range(2):
        rows = slice(half * half_rows, (half + 1) * half_rows)
        partial_rows = jnp.zeros((half_rows, width), jnp.float32)
        for which in range(expert_count):
            gate_masked = gate_g[rows] * masks[which][rows]
            up_masked = up_g[rows] * masks[which][rows]
            partial_rows = (
                partial_rows
                + contract_cols(gate_masked, w_gate[which])
                + contract_cols(up_masked, w_up[which])
            )
        pieces = lax.all_to_all(
            partial_rows.reshape(N_TP, rows_dev, width), TP, split_axis=0, concat_axis=0, tiled=True
        )
        summed.append(jnp.sum(pieces, axis=0))
    cols = []
    for parity in range(2):
        got = [lax.ppermute(summed[half], AXES, deliver_perm(half, parity)) for half in range(2)]
        cols.append(got[0] + got[1])
    input_grad = jnp.concatenate(cols, axis=1).astype(jnp.bfloat16)
    return (
        input_grad,
        gate_total.astype(jnp.bfloat16),
        up_total.astype(jnp.bfloat16),
        down_total.astype(jnp.bfloat16),
    )


def solution(mesh):
    fine = Mesh(mesh.devices.reshape(SIZES), AXES)
    return jax.shard_map(
        shards,
        mesh=fine,
        in_specs=(
            P(DP, None),
            P(DP, None),
            P(DP, TP),
            P(DP, TP),
            P(None, DP, TP),
            P(None, DP, TP),
            P(None, TP, DP),
            P(DP),
            P(),
        ),
        out_specs=(
            P(DP, TP),
            P(None, DP, TP),
            P(None, DP, TP),
            P(None, TP, DP),
        ),
        check_vma=False,
    )
```

```python
import numpy as np
import jax
import jax.numpy as jnp
from jax import lax
from jax.sharding import Mesh
from jax.sharding import PartitionSpec as P

BLOCK = 128
AXES = ("x", "ylo", "core", "z", "yhi")
SIZES = (4, 2, 2, 4, 2)
DP = ("x", "ylo", "core")
TP = ("z", "yhi")
CHIPS = ("x", "ylo")
N_DP = 16
N_TP = 8


def rank_of_pos(pos):
    core, x, ylo = pos // 8, (pos % 8) // 2, pos % 2
    return x * 4 + ylo * 2 + core


POS_RANK = np.array([rank_of_pos(p) for p in range(N_DP)], np.int32)


def deliver_perm(k):
    pairs = []
    for i in range(N_DP):
        for t in range(N_TP):
            dest = 8 * ((i % 2) ^ k) + t
            pairs.append((i * N_TP + t, dest * N_TP + i // 2))
    return pairs


def contract_rows(left_op, right_op):
    return lax.dot_general(
        left_op, right_op, (((0,), (0,)), ((), ())), preferred_element_type=jnp.float32
    )


def contract_cols(left_op, right_op):
    return lax.dot_general(
        left_op, right_op, (((1,), (1,)), ((), ())), preferred_element_type=jnp.float32
    )


def expert_masks(block_expert, row_count, expert_count):
    spread = jnp.broadcast_to(block_expert[:, None], (row_count // BLOCK, BLOCK)).reshape(
        row_count, 1
    )
    return [(spread == which).astype(jnp.bfloat16) for which in range(expert_count)]


def to_gathered_order(cols):
    width = cols.shape[1]
    return cols.reshape(4, 2, 2, BLOCK, width).transpose(2, 0, 1, 3, 4).reshape(-1, width)


def shards(rows_in, out_grad, gate_pre, up_pre, w_gate, w_up, w_down, live_rows, block_expert):
    rows_dev = rows_in.shape[0]
    expert_count = w_gate.shape[0]
    ff = gate_pre.shape[1]
    dy_cols = lax.all_to_all(out_grad, DP, split_axis=1, concat_axis=0, tiled=True)
    row_count = dy_cols.shape[0]
    expert_g = jnp.take(block_expert, jnp.asarray(POS_RANK), axis=0)
    masks_g = expert_masks(expert_g, row_count, expert_count)
    masks = expert_masks(block_expert, row_count, expert_count)

    positions = jnp.arange(rows_dev, dtype=jnp.int32)[:, None]
    row_mask = (positions < live_rows[0]).astype(jnp.float32)
    gate_vals = gate_pre.astype(jnp.float32)
    up_vals = up_pre.astype(jnp.float32)
    sigmoid = jax.nn.sigmoid(gate_vals)
    silu_vals = gate_vals * sigmoid
    hidden = (silu_vals * up_vals * row_mask).astype(jnp.bfloat16)
    hid_g = lax.all_gather(hidden, DP, axis=0, tiled=True)

    dy_g = to_gathered_order(dy_cols)
    result = jnp.zeros((row_count, ff), jnp.float32)
    for which in range(expert_count):
        result = result + contract_cols(dy_g * masks_g[which], w_down[which])
    hid_g, result = lax.optimization_barrier((hid_g, result))
    result = lax.psum_scatter(
        result.reshape(2, row_count // 2, ff), "core", scatter_dimension=0, tiled=True
    ).reshape(N_DP // 2, rows_dev, ff)
    pieces = lax.all_to_all(result, CHIPS, split_axis=0, concat_axis=0, tiled=True)
    hidden_grad = jnp.sum(pieces, axis=0)
    rows_in, hidden_grad = lax.optimization_barrier((rows_in, hidden_grad))
    x_cols = lax.all_to_all(rows_in, DP, split_axis=1, concat_axis=0, tiled=True)

    up_grad = (hidden_grad * silu_vals * row_mask).astype(jnp.bfloat16)
    gate_grad = (
        hidden_grad * up_vals * sigmoid * (1.0 + gate_vals * (1.0 - sigmoid)) * row_mask
    ).astype(jnp.bfloat16)
    packed = jnp.stack([gate_grad, up_grad], axis=1)
    packed = lax.all_gather(packed, DP, axis=0, tiled=True)
    both = packed.reshape(row_count, 2 * ff)

    down_terms = []
    gate_terms = []
    up_terms = []
    for which in range(expert_count):
        down_terms.append(contract_rows(hid_g * masks[which], dy_cols))
        weight_grads = contract_rows(x_cols, both * masks[which])
        gate_terms.append(weight_grads[:, :ff])
        up_terms.append(weight_grads[:, ff:])
    down_total = jnp.stack(down_terms, 0)
    gate_total = jnp.stack(gate_terms, 0)
    up_total = jnp.stack(up_terms, 0)

    width = w_gate.shape[1]
    half_rows = row_count // 2
    w_both = [jnp.concatenate([w_gate[which], w_up[which]], axis=1) for which in range(expert_count)]
    summed = []
    for half in range(2):
        rows = slice(half * half_rows, (half + 1) * half_rows)
        partial_rows = jnp.zeros((half_rows, width), jnp.float32)
        for which in range(expert_count):
            partial_rows = partial_rows + contract_cols(
                both[rows] * masks[which][rows], w_both[which]
            )
        pieces = lax.all_to_all(
            partial_rows.reshape(N_TP, rows_dev, width), TP, split_axis=0, concat_axis=0, tiled=True
        )
        summed.append(jnp.sum(pieces, axis=0))
    summed = jnp.stack(summed, 0)
    core = lax.axis_index("core")
    low = lax.axis_index("x") < 2
    got = []
    for k in range(2):
        piece = lax.dynamic_index_in_dim(summed, core ^ k, 0, keepdims=False)
        got.append(lax.ppermute(piece, AXES, deliver_perm(k)))
    first = jnp.where(low, got[0], got[1])
    second = jnp.where(low, got[1], got[0])
    input_grad = jnp.concatenate([first, second], axis=1).astype(jnp.bfloat16)
    return (
        input_grad,
        gate_total.astype(jnp.bfloat16),
        up_total.astype(jnp.bfloat16),
        down_total.astype(jnp.bfloat16),
    )


def solution(mesh):
    fine = Mesh(mesh.devices.reshape(SIZES), AXES)
    return jax.shard_map(
        shards,
        mesh=fine,
        in_specs=(
            P(DP, None),
            P(DP, None),
            P(DP, TP),
            P(DP, TP),
            P(None, DP, TP),
            P(None, DP, TP),
            P(None, TP, DP),
            P(DP),
            P(),
        ),
        out_specs=(
            P(DP, TP),
            P(None, DP, TP),
            P(None, DP, TP),
            P(None, TP, DP),
        ),
        check_vma=False,
    )
```

```python
import numpy as np
import jax
import jax.numpy as jnp
from jax import lax
from jax.sharding import Mesh
from jax.sharding import PartitionSpec as P

BLOCK = 128
AXES = ("x", "ylo", "core", "z", "yhi")
SIZES = (4, 2, 2, 4, 2)
DP = ("x", "ylo", "core")
TP = ("z", "yhi")
CHIPS = ("x", "ylo")
N_DP = 16
N_TP = 8


def rank_of_pos(pos):
    core, x, ylo = pos // 8, (pos % 8) // 2, pos % 2
    return x * 4 + ylo * 2 + core


POS_RANK = np.array([rank_of_pos(p) for p in range(N_DP)], np.int32)


def deliver_perm(k):
    pairs = []
    for i in range(N_DP):
        for t in range(N_TP):
            dest = 8 * ((i % 2) ^ k) + t
            pairs.append((i * N_TP + t, dest * N_TP + i // 2))
    return pairs


def contract_rows(left_op, right_op):
    return lax.dot_general(
        left_op, right_op, (((0,), (0,)), ((), ())), preferred_element_type=jnp.float32
    )


def contract_cols(left_op, right_op):
    return lax.dot_general(
        left_op, right_op, (((1,), (1,)), ((), ())), preferred_element_type=jnp.float32
    )


def expert_masks(block_expert, row_count, expert_count):
    spread = jnp.broadcast_to(block_expert[:, None], (row_count // BLOCK, BLOCK)).reshape(
        row_count, 1
    )
    return [(spread == which).astype(jnp.bfloat16) for which in range(expert_count)]


def to_gathered_order(cols):
    width = cols.shape[1]
    return cols.reshape(4, 2, 2, BLOCK, width).transpose(2, 0, 1, 3, 4).reshape(-1, width)


def shards(rows_in, out_grad, gate_pre, up_pre, w_gate, w_up, w_down, live_rows, block_expert):
    rows_dev = rows_in.shape[0]
    expert_count = w_gate.shape[0]
    ff = gate_pre.shape[1]
    dy_cols = lax.all_to_all(out_grad, DP, split_axis=1, concat_axis=0, tiled=True)
    row_count = dy_cols.shape[0]
    expert_g = jnp.take(block_expert, jnp.asarray(POS_RANK), axis=0)
    masks_g = expert_masks(expert_g, row_count, expert_count)
    masks = expert_masks(block_expert, row_count, expert_count)

    positions = jnp.arange(rows_dev, dtype=jnp.int32)[:, None]
    row_mask = (positions < live_rows[0]).astype(jnp.float32)
    gate_vals = gate_pre.astype(jnp.float32)
    up_vals = up_pre.astype(jnp.float32)
    sigmoid = jax.nn.sigmoid(gate_vals)
    silu_vals = gate_vals * sigmoid
    hidden = (silu_vals * up_vals * row_mask).astype(jnp.bfloat16)
    hid_g = lax.all_gather(hidden, DP, axis=0, tiled=True)

    dy_g = to_gathered_order(dy_cols)
    result = jnp.zeros((row_count, ff), jnp.float32)
    for which in range(expert_count):
        result = result + contract_cols(dy_g * masks_g[which], w_down[which])
    hid_g, result = lax.optimization_barrier((hid_g, result))
    result = lax.psum_scatter(
        result.reshape(2, row_count // 2, ff), "core", scatter_dimension=0, tiled=True
    ).reshape(N_DP // 2, rows_dev, ff)
    pieces = lax.all_to_all(result, CHIPS, split_axis=0, concat_axis=0, tiled=True)
    hidden_grad = jnp.sum(pieces, axis=0)
    rows_in, hidden_grad = lax.optimization_barrier((rows_in, hidden_grad))
    x_cols = lax.all_to_all(rows_in, DP, split_axis=1, concat_axis=0, tiled=True)

    up_grad = (hidden_grad * silu_vals * row_mask).astype(jnp.bfloat16)
    gate_grad = (
        hidden_grad * up_vals * sigmoid * (1.0 + gate_vals * (1.0 - sigmoid)) * row_mask
    ).astype(jnp.bfloat16)
    packed = jnp.stack([gate_grad, up_grad], axis=1)
    packed = lax.all_gather(packed, DP, axis=0, tiled=True)
    gate_g, up_g = packed[:, 0], packed[:, 1]

    down_terms = []
    gate_terms = []
    up_terms = []
    for which in range(expert_count):
        down_terms.append(contract_rows(hid_g, dy_cols * masks[which]))
        x_masked = x_cols * masks[which]
        gate_terms.append(contract_rows(x_masked, gate_g))
        up_terms.append(contract_rows(x_masked, up_g))
    down_total = jnp.stack(down_terms, 0)
    gate_total = jnp.stack(gate_terms, 0)
    up_total = jnp.stack(up_terms, 0)

    width = w_gate.shape[1]
    half_rows = row_count // 2
    summed = []
    for half in range(2):
        rows = slice(half * half_rows, (half + 1) * half_rows)
        partial_rows = jnp.zeros((half_rows, width), jnp.float32)
        for which in range(expert_count):
            gate_masked = gate_g[rows] * masks[which][rows]
            up_masked = up_g[rows] * masks[which][rows]
            partial_rows = (
                partial_rows
                + contract_cols(gate_masked, w_gate[which])
                + contract_cols(up_masked, w_up[which])
            )
        pieces = lax.all_to_all(
            partial_rows.reshape(N_TP, rows_dev, width), TP, split_axis=0, concat_axis=0, tiled=True
        )
        summed.append(jnp.sum(pieces, axis=0))
    summed = jnp.stack(summed, 0)
    core = lax.axis_index("core")
    low = lax.axis_index("x") < 2
    got = []
    for k in range(2):
        piece = lax.dynamic_index_in_dim(summed, core ^ k, 0, keepdims=False)
        got.append(lax.ppermute(piece, AXES, deliver_perm(k)))
    first = jnp.where(low, got[0], got[1])
    second = jnp.where(low, got[1], got[0])
    input_grad = jnp.concatenate([first, second], axis=1).astype(jnp.bfloat16)
    return (
        input_grad,
        gate_total.astype(jnp.bfloat16),
        up_total.astype(jnp.bfloat16),
        down_total.astype(jnp.bfloat16),
    )


def solution(mesh):
    fine = Mesh(mesh.devices.reshape(SIZES), AXES)
    return jax.shard_map(
        shards,
        mesh=fine,
        in_specs=(
            P(DP, None),
            P(DP, None),
            P(DP, TP),
            P(DP, TP),
            P(None, DP, TP),
            P(None, DP, TP),
            P(None, TP, DP),
            P(DP),
            P(),
        ),
        out_specs=(
            P(DP, TP),
            P(None, DP, TP),
            P(None, DP, TP),
            P(None, TP, DP),
        ),
        check_vma=False,
    )
```

```python
import numpy as np
import jax
import jax.numpy as jnp
from jax import lax
from jax.sharding import Mesh
from jax.sharding import PartitionSpec as P

BLOCK = 128
AXES = ("x", "ylo", "core", "z", "yhi")
SIZES = (4, 2, 2, 4, 2)
DP = ("x", "ylo", "core")
TP = ("z", "yhi")
CHIPS = ("x", "ylo")
N_DP = 16
N_TP = 8


def rank_of_pos(pos):
    core, x, ylo = pos // 8, (pos % 8) // 2, pos % 2
    return x * 4 + ylo * 2 + core


POS_RANK = np.array([rank_of_pos(p) for p in range(N_DP)], np.int32)


def deliver_perm(k):
    pairs = []
    for i in range(N_DP):
        for t in range(N_TP):
            dest = 8 * ((i % 2) ^ k) + t
            pairs.append((i * N_TP + t, dest * N_TP + i // 2))
    return pairs


def contract_rows(left_op, right_op):
    return lax.dot_general(
        left_op, right_op, (((0,), (0,)), ((), ())), preferred_element_type=jnp.float32
    )


def contract_cols(left_op, right_op):
    return lax.dot_general(
        left_op, right_op, (((1,), (1,)), ((), ())), preferred_element_type=jnp.float32
    )


def expert_masks(block_expert, row_count, expert_count):
    spread = jnp.broadcast_to(block_expert[:, None], (row_count // BLOCK, BLOCK)).reshape(
        row_count, 1
    )
    return [(spread == which).astype(jnp.bfloat16) for which in range(expert_count)]


def to_gathered_order(cols):
    width = cols.shape[1]
    return cols.reshape(4, 2, 2, BLOCK, width).transpose(2, 0, 1, 3, 4).reshape(-1, width)


def shards(rows_in, out_grad, gate_pre, up_pre, w_gate, w_up, w_down, live_rows, block_expert):
    rows_dev = rows_in.shape[0]
    expert_count = w_gate.shape[0]
    ff = gate_pre.shape[1]
    dy_cols = lax.all_to_all(out_grad, DP, split_axis=1, concat_axis=0, tiled=True)
    row_count = dy_cols.shape[0]
    expert_g = jnp.take(block_expert, jnp.asarray(POS_RANK), axis=0)
    masks_g = expert_masks(expert_g, row_count, expert_count)
    masks = expert_masks(block_expert, row_count, expert_count)

    positions = jnp.arange(rows_dev, dtype=jnp.int32)[:, None]
    row_mask = (positions < live_rows[0]).astype(jnp.float32)
    gate_vals = gate_pre.astype(jnp.float32)
    up_vals = up_pre.astype(jnp.float32)
    sigmoid = jax.nn.sigmoid(gate_vals)
    silu_vals = gate_vals * sigmoid
    hidden = (silu_vals * up_vals * row_mask).astype(jnp.bfloat16)
    hid_g = lax.all_gather(hidden, DP, axis=0, tiled=True)

    dy_g = to_gathered_order(dy_cols)
    result = jnp.zeros((row_count, ff), jnp.float32)
    for which in range(expert_count):
        result = result + contract_cols(dy_g * masks_g[which], w_down[which])
    hid_g, result = lax.optimization_barrier((hid_g, result))
    result = lax.psum_scatter(
        result.reshape(2, row_count // 2, ff), "core", scatter_dimension=0, tiled=True
    ).reshape(N_DP // 2, rows_dev, ff)
    pieces = lax.all_to_all(result, CHIPS, split_axis=0, concat_axis=0, tiled=True)
    hidden_grad = jnp.sum(pieces, axis=0)
    rows_in, hidden_grad = lax.optimization_barrier((rows_in, hidden_grad))
    x_cols = lax.all_to_all(rows_in, DP, split_axis=1, concat_axis=0, tiled=True)

    up_grad = (hidden_grad * silu_vals * row_mask).astype(jnp.bfloat16)
    gate_grad = (
        hidden_grad * up_vals * sigmoid * (1.0 + gate_vals * (1.0 - sigmoid)) * row_mask
    ).astype(jnp.bfloat16)
    packed = jnp.stack([gate_grad, up_grad], axis=1)
    packed = lax.all_gather(packed, DP, axis=0, tiled=True)
    gate_g, up_g = packed[:, 0], packed[:, 1]

    down_terms = []
    gate_terms = []
    up_terms = []
    for which in range(expert_count):
        down_terms.append(contract_rows(hid_g, dy_cols * masks[which]))
        x_masked = x_cols * masks[which]
        gate_terms.append(contract_rows(x_masked, gate_g))
        up_terms.append(contract_rows(x_masked, up_g))
    down_total = jnp.stack(down_terms, 0)
    gate_total = jnp.stack(gate_terms, 0)
    up_total = jnp.stack(up_terms, 0)

    width = w_gate.shape[1]
    half_rows = row_count // 2
    summed = []
    for half in range(2):
        rows = slice(half * half_rows, (half + 1) * half_rows)
        partial_rows = jnp.zeros((half_rows, width), jnp.float32)
        for which in range(expert_count):
            partial_rows = partial_rows + masks[which][rows].astype(jnp.float32) * (
                contract_cols(gate_g[rows], w_gate[which]) + contract_cols(up_g[rows], w_up[which])
            )
        pieces = lax.all_to_all(
            partial_rows.reshape(N_TP, rows_dev, width), TP, split_axis=0, concat_axis=0, tiled=True
        )
        summed.append(jnp.sum(pieces, axis=0))
    summed = jnp.stack(summed, 0)
    core = lax.axis_index("core")
    low = lax.axis_index("x") < 2
    got = []
    for k in range(2):
        piece = lax.dynamic_index_in_dim(summed, core ^ k, 0, keepdims=False)
        got.append(lax.ppermute(piece, AXES, deliver_perm(k)))
    first = jnp.where(low, got[0], got[1])
    second = jnp.where(low, got[1], got[0])
    input_grad = jnp.concatenate([first, second], axis=1).astype(jnp.bfloat16)
    return (
        input_grad,
        gate_total.astype(jnp.bfloat16),
        up_total.astype(jnp.bfloat16),
        down_total.astype(jnp.bfloat16),
    )


def solution(mesh):
    fine = Mesh(mesh.devices.reshape(SIZES), AXES)
    return jax.shard_map(
        shards,
        mesh=fine,
        in_specs=(
            P(DP, None),
            P(DP, None),
            P(DP, TP),
            P(DP, TP),
            P(None, DP, TP),
            P(None, DP, TP),
            P(None, TP, DP),
            P(DP),
            P(),
        ),
        out_specs=(
            P(DP, TP),
            P(None, DP, TP),
            P(None, DP, TP),
            P(None, TP, DP),
        ),
        check_vma=False,
    )
```
